128 devices in a mesh: req: 32 (over z, y, x_lo), tp: 4 (over x_hi, core).
Axes of the slice: x: 4 (x_hi: 2, x_lo: 2; x = x_hi * 2 + x_lo), y: 4, z: 4, core: 2. Of those that a mesh axis runs over, the one named last changes fastest.
Arguments:
- tokens: bfloat16 [16384, 4096], P('req', 'tp'), may hold values from -400 to 400
- input_norm_gain: float32 [4096], replicated, may hold values from 0.1 to 1.9
- query_weight: bfloat16 [4096, 2048], P(None, 'tp'), may hold values from -0.078125 to 0.078125
- key_weight: bfloat16 [4096, 2048], P(None, 'tp'), may hold values from -1.953125 to 1.953125
- value_weight: bfloat16 [4096, 2048], P(None, 'tp'), may hold values from -0.09375 to 0.09375
- query_down_maps: bfloat16 [4096, 512], replicated, may hold values from -0.09375 to 0.09375
- value_down_maps: bfloat16 [4096, 512], replicated, may hold values from -0.09375 to 0.09375
- query_up_maps: bfloat16 [512, 2048], P(None, 'tp'), may hold values from -1.5 to 1.5
- value_up_maps: bfloat16 [512, 2048], P(None, 'tp'), may hold values from -1.5 to 1.5
- lengths: int32 [16], replicated, may hold values from 1 to 8448, 16384 in all
- prompt_adapter_index: int32 [16], replicated, may hold values from 0 to 31
Outputs:
- attended: bfloat16 [16384, 2048], P('req', 'tp')
The draws below stay inside these ranges and needn't reach their ends.
Inputs may be any that keep to these rules, and one draw needn't show every extreme that they name: `lengths`: the longest prompt has exactly 8448 tokens.
All inputs are finite; a program needn't handle non-finite values.
Results may differ from the reference program's by a relative error of at most 0.0083.
Values may be sent and summed in bfloat16 or wider, within the bound.
No kernel may reach another device: no remote copies, remote signals or barrier semaphores. Data moves between devices by JAX's collectives and lax.ppermute only.
A program may use at most 192 MiB of HBM per device.

```python
import math
import jax
import jax.numpy as jnp
import numpy as np
from jax import lax

INPUT_WIDTH = 4096
HEADS = 16
HEAD = 128
ADAPTER_RANK = 16
ADAPTER_COUNT = 32
TOK_DEV = 512
HEAD_FEATURES = 2048
TOKENS = 16384
REQS = 16
MAXLEN = 8448


def weight_common(key):
    return jnp.clip(jax.random.normal(key, (INPUT_WIDTH, HEAD_FEATURES), jnp.float32), -5.0, 5.0) / math.sqrt(INPUT_WIDTH)


def draw_query_weight(key, part):
    return weight_common(jax.random.fold_in(key, 11)).astype(jnp.bfloat16)


def draw_key_weight(key, part):
    return weight_common(jax.random.fold_in(key, 12)).astype(jnp.bfloat16)


def draw_tokens(key, part):
    base_key = jax.random.fold_in(key, 21)
    feature_key = jax.random.fold_in(key, 22)
    row_key = jax.random.fold_in(key, 23)
    feature_scale = jnp.exp(jax.random.uniform(feature_key, (INPUT_WIDTH,), jnp.float32) * math.log(10.0))
    row_scale = jnp.exp(jax.random.uniform(row_key, (TOKENS, 1), jnp.float32) * math.log(10.0))
    base = jnp.clip(jax.random.normal(base_key, (TOKENS, INPUT_WIDTH), jnp.float32), -4.0, 4.0)
    return (base * feature_scale[None, :] * row_scale).astype(jnp.bfloat16)


def with_ends(drawn, key, smallest, high):
    extent = drawn.shape
    place = [jax.random.randint(jax.random.fold_in(key, axis), (), 0, extent[axis]) for axis in range(len(extent))]
    drawn = drawn.at[tuple(place)].set(smallest)
    longest = extent.index(max(extent))
    place[longest] = (place[longest] + 1) % extent[longest]
    return drawn.at[tuple(place)].set(high)


def block_levels(own_key, shape, pieces, smallest, high):
    level, own = 1.0, jax.random.fold_in(own_key, 6)
    for dim, parts in pieces:
        draws = jnp.exp(jax.random.uniform(jax.random.fold_in(own, dim), (parts,), jnp.float32, smallest / len(pieces), high / len(pieces)))
        level = level * jnp.repeat(draws, shape[dim] // parts).reshape([-1 if axis == dim else 1 for axis in range(len(shape))])
    return level


def split_up(count, total, reach, skew):
    weights = [(1 << 20) // math.isqrt(standing ** skew) + 1 for standing in range(2, count + 1)]
    surplus, counts = total - reach - (count - 1), [1] * (count - 1)
    while surplus > 0:
        free = [i for i in range(count - 1) if counts[i] < reach]
        whole, budget = sum([weights[i] for i in free]), surplus
        for i in free:
            addition = min(reach - counts[i], max(1, budget * weights[i] // whole), surplus)
            counts[i] = counts[i] + addition
            surplus = surplus - addition
    return np.array([reach] + counts)


def uneven_parts(own_key, number_of, total, bound, slope):
    if number_of == 2:
        one = jax.random.randint(own_key, (), max(1, total - bound), min(bound, total - 1) + 1)
        return jnp.stack([one, total - one])
    sizes = jnp.asarray(split_up(number_of, total, bound, slope), jnp.int32)
    twos = (number_of - 1) // 2
    donor, sink = sizes[1:1 + 2 * twos:2], sizes[2:2 + 2 * twos:2]
    slack = jnp.minimum(donor - 1, bound - sink)
    passed = jax.random.randint(jax.random.fold_in(own_key, 1), (twos,), 0, 1 << 20) % (slack + 1)
    sizes = sizes.at[1:1 + 2 * twos:2].set(donor - passed).at[2:2 + 2 * twos:2].set(sink + passed)
    return sizes[jax.random.permutation(jax.random.fold_in(own_key, 2), number_of)]


def noise(own_key, shape, scale, most, pieces=(), kind=jnp.bfloat16):
    drawn = scale * jax.random.normal(own_key, shape, jnp.float32)
    if pieces:
        drawn = drawn * block_levels(own_key, shape, pieces, -0.22, 0.18)
    return jnp.clip(drawn, -most, most).astype(kind)


def setup_inputs(seed: int = 0) -> dict:
    seeds = jax.random.split(jax.random.key(seed), 12)
    tokens = draw_tokens(jax.random.fold_in(seeds[11], 71), 0)
    input_norm_gain = jnp.clip(1.0 + 0.18 * jax.random.normal(seeds[1], (INPUT_WIDTH,), jnp.float32), 0.1, 1.9)
    query_weight = draw_query_weight(jax.random.fold_in(seeds[11], 71), 0)
    key_weight = draw_key_weight(jax.random.fold_in(seeds[11], 71), 0)
    value_weight = noise(seeds[4], (INPUT_WIDTH, HEAD_FEATURES), INPUT_WIDTH ** -0.5, 0.09375, ((1, 4),))
    query_down_maps = noise(seeds[5], (INPUT_WIDTH, ADAPTER_COUNT * ADAPTER_RANK), INPUT_WIDTH ** -0.5, 0.09375)
    value_down_maps = noise(seeds[6], (INPUT_WIDTH, ADAPTER_COUNT * ADAPTER_RANK), INPUT_WIDTH ** -0.5, 0.09375)
    query_up_maps = noise(seeds[7], (ADAPTER_COUNT * ADAPTER_RANK, HEAD_FEATURES), ADAPTER_RANK ** -0.5, 1.5, ((1, 4),))
    value_up_maps = noise(seeds[8], (ADAPTER_COUNT * ADAPTER_RANK, HEAD_FEATURES), ADAPTER_RANK ** -0.5, 1.5, ((1, 4),))
    lengths = uneven_parts(seeds[9], REQS, TOKENS, MAXLEN, 2).astype(jnp.int32)
    prompt_adapter_index = with_ends(jax.random.randint(seeds[10], (REQS,), 0, ADAPTER_COUNT), jax.random.fold_in(seeds[10], 1), 0, ADAPTER_COUNT - 1).astype(jnp.int32)
    return {"tokens": tokens, "input_norm_gain": input_norm_gain, "query_weight": query_weight, "key_weight": key_weight, "value_weight": value_weight, "query_down_maps": query_down_maps, "value_down_maps": value_down_maps, "query_up_maps": query_up_maps, "value_up_maps": value_up_maps, "lengths": lengths, "prompt_adapter_index": prompt_adapter_index}


EPS = 1e-05
ADAPTER_SCALE = 0.5
MASKED = -1e+30

def prompt_layout(lengths, positions):
    ends = jnp.cumsum(lengths).astype(jnp.int32)
    before = (ends[None, :] <= positions[:, None]).astype(jnp.int32)
    starts = lax.optimization_barrier(jnp.sum(before * lengths[None, :], axis=1)).astype(jnp.int32)
    prompt = lax.optimization_barrier(jnp.sum(before, axis=1)).astype(jnp.int32)
    return (starts, prompt)

def adapter_mask(prompt, prompt_adapter_index, count, rank):
    chosen = (prompt[:, None] == jnp.arange(prompt_adapter_index.shape[0], dtype=jnp.int32)[None, :]).astype(jnp.int32)
    adapter = lax.optimization_barrier(jnp.sum(chosen * prompt_adapter_index[None, :], axis=1)).astype(jnp.int32)
    column = jnp.arange(count * rank, dtype=jnp.int32) // rank
    return (column[None, :] == adapter[:, None]).astype(jnp.float32)

def rotate(field, offsets, width):
    half = width // 2
    freq = jnp.exp(jnp.arange(half, dtype=jnp.float32) * (-2.0 * math.log(10000.0) / width))
    angle = offsets.astype(jnp.float32)[:, None] * freq[None, :]
    cosine = jnp.cos(angle)[:, None, :]
    sine = jnp.sin(angle)[:, None, :]
    first = field[..., :half]
    second = field[..., half:]
    return jnp.concatenate([first * cosine - second * sine, second * cosine + first * sine], axis=-1)

def reference(tokens, input_norm_gain, query_weight, key_weight, value_weight, query_down_maps, value_down_maps, query_up_maps, value_up_maps, lengths, prompt_adapter_index):
    positions = jnp.arange(TOKENS, dtype=jnp.int32)
    starts, prompt = prompt_layout(lengths, positions)
    causal_mask = adapter_mask(prompt, prompt_adapter_index, ADAPTER_COUNT, ADAPTER_RANK)
    tok_float = tokens.astype(jnp.float32)
    normed = (tok_float * lax.rsqrt(lax.optimization_barrier(jnp.mean(tok_float * tok_float, axis=1, keepdims=True)) + EPS) * input_norm_gain[None, :]).astype(jnp.bfloat16)

    def apply_projection(weight):
        return jnp.dot(normed, weight, preferred_element_type=jnp.float32)
    query_middle = (apply_projection(query_down_maps) * causal_mask).astype(jnp.bfloat16)
    value_middle = (apply_projection(value_down_maps) * causal_mask).astype(jnp.bfloat16)
    query_linear = apply_projection(query_weight) + ADAPTER_SCALE * jnp.dot(query_middle, query_up_maps, preferred_element_type=jnp.float32)
    key_lin = apply_projection(key_weight)
    value_rows = (apply_projection(value_weight) + ADAPTER_SCALE * jnp.dot(value_middle, value_up_maps, preferred_element_type=jnp.float32)).astype(jnp.bfloat16)
    offsets = positions - starts
    queries = rotate(query_linear.reshape(TOKENS, HEADS, HEAD), offsets, HEAD).astype(jnp.bfloat16)
    keys = rotate(key_lin.reshape(TOKENS, HEADS, HEAD), offsets, HEAD).astype(jnp.bfloat16)
    value_rows = value_rows.reshape(TOKENS, HEADS, HEAD)
    padding = jnp.zeros((MAXLEN, HEADS, HEAD), jnp.bfloat16)
    keys_pad = jnp.concatenate([padding, keys], axis=0)
    values_pad = jnp.concatenate([padding, value_rows], axis=0)
    scale = 1.0 / math.sqrt(HEAD)

    def block(index):
        first = (index * TOK_DEV).astype(jnp.int32)
        query_block = lax.dynamic_slice_in_dim(queries, first, TOK_DEV, 0).astype(jnp.float32)
        key_block = lax.dynamic_slice_in_dim(keys_pad, first, MAXLEN + TOK_DEV, 0).astype(jnp.float32)
        value_block = lax.dynamic_slice_in_dim(values_pad, first, MAXLEN + TOK_DEV, 0).astype(jnp.float32)
        query_pos = first + jnp.arange(TOK_DEV, dtype=jnp.int32)
        query_start = lax.dynamic_slice_in_dim(starts, first, TOK_DEV, 0)
        key_pos = first - MAXLEN + jnp.arange(MAXLEN + TOK_DEV, dtype=jnp.int32)
        allowed = (key_pos[None, :] >= query_start[:, None]) & (key_pos[None, :] <= query_pos[:, None])
        scores = jnp.einsum('qhd,khd->hqk', query_block, key_block, precision=lax.Precision.HIGHEST) * scale
        scores = jnp.where(allowed[None], scores, MASKED)
        peak = lax.optimization_barrier(jnp.max(scores, axis=2, keepdims=True))
        weights = jnp.where(allowed[None], jnp.exp(scores - peak), 0.0)
        total = lax.optimization_barrier(jnp.sum(weights, axis=2))
        rounded = lax.optimization_barrier(weights.astype(jnp.bfloat16)).astype(jnp.float32)
        summed = jnp.einsum('hqk,khd->qhd', rounded, value_block, precision=lax.Precision.HIGHEST)
        return (summed / jnp.transpose(total)[:, :, None]).reshape(TOK_DEV, HEADS * HEAD).astype(jnp.bfloat16)
    result = lax.map(block, jnp.arange(TOKENS // TOK_DEV, dtype=jnp.int32))
    return result.reshape(TOKENS, HEADS * HEAD)
```

```python
import functools
import math

import jax
import jax.numpy as jnp
from jax import lax
from jax.sharding import PartitionSpec as P

HEAD = 128
ADAPTER_RANK = 16
ADAPTER_COUNT = 32


EPS = 1e-05
ADAPTER_SCALE = 0.5
MASKED = -1e30


def prompt_layout(lengths, positions):
    ends = jnp.cumsum(lengths)
    before = (ends[None, :] <= positions[:, None]).astype(jnp.int32)
    starts = jnp.sum(before * lengths[None, :], axis=1)
    prompt = jnp.sum(before, axis=1)
    return (starts, prompt)


def adapter_mask(prompt, prompt_adapter_index, count, rank):
    chosen = (
        prompt[:, None] == jnp.arange(prompt_adapter_index.shape[0], dtype=jnp.int32)[None, :]
    ).astype(jnp.int32)
    adapter = jnp.sum(chosen * prompt_adapter_index[None, :], axis=1)
    column = jnp.arange(count * rank, dtype=jnp.int32) // rank
    return (column[None, :] == adapter[:, None]).astype(jnp.float32)


def rotate(field, offsets, width):
    half = width // 2
    freq = jnp.exp(jnp.arange(half, dtype=jnp.float32) * (-2.0 * math.log(10000.0) / width))
    angle = offsets.astype(jnp.float32)[:, None] * freq[None, :]
    cosine = jnp.cos(angle)[:, None, :]
    sine = jnp.sin(angle)[:, None, :]
    first = field[..., :half]
    second = field[..., half:]
    return jnp.concatenate(
        [first * cosine - second * sine, second * cosine + first * sine], axis=-1
    )


MAXLEN = 8448


def body(
    req_count,
    tokens,
    input_norm_gain,
    query_weight,
    key_weight,
    value_weight,
    query_down_maps,
    value_down_maps,
    query_up_maps,
    value_up_maps,
    lengths,
    prompt_adapter_index,
):
    row_count = tokens.shape[0]
    window = min(req_count - 1, -(-(MAXLEN - 1) // row_count))
    req_index = lax.axis_index("req")
    positions = req_index * row_count + jnp.arange(row_count, dtype=jnp.int32)
    starts, prompt = prompt_layout(lengths, positions)
    causal_mask = adapter_mask(prompt, prompt_adapter_index, ADAPTER_COUNT, ADAPTER_RANK)
    incoming_weights = (query_weight, key_weight, value_weight, query_down_maps, value_down_maps)
    whole = lax.all_gather(tokens, "tp", axis=1, tiled=True)
    whole_float = whole.astype(jnp.float32)
    normed = (
        whole_float
        * lax.rsqrt(jnp.mean(whole_float * whole_float, axis=1, keepdims=True) + EPS)
        * input_norm_gain[None, :]
    ).astype(jnp.bfloat16)
    projected = tuple(
        (jnp.dot(normed, weight, preferred_element_type=jnp.float32) for weight in incoming_weights)
    )
    query_linear, key_lin, value_linear, query_middle, value_middle = projected
    query_middle = (query_middle * causal_mask).astype(jnp.bfloat16)
    value_middle = (value_middle * causal_mask).astype(jnp.bfloat16)
    query_linear = query_linear + ADAPTER_SCALE * jnp.dot(
        query_middle, query_up_maps, preferred_element_type=jnp.float32
    )
    value_rows = (
        value_linear
        + ADAPTER_SCALE * jnp.dot(value_middle, value_up_maps, preferred_element_type=jnp.float32)
    ).astype(jnp.bfloat16)
    head_count = query_linear.shape[1] // HEAD
    offsets = positions - starts
    queries = jnp.transpose(
        rotate(query_linear.reshape(row_count, head_count, HEAD), offsets, HEAD).astype(
            jnp.bfloat16
        ),
        (1, 0, 2),
    )
    keys = (
        rotate(key_lin.reshape(row_count, head_count, HEAD), offsets, HEAD)
        .astype(jnp.bfloat16)
        .reshape(row_count, head_count * HEAD)
    )
    key_value = jnp.stack([keys, value_rows])
    scale = 1.0 / math.sqrt(HEAD)

    def attend(state, block, key_first):
        peak, total, summed = state
        block_rows = block.shape[1]
        key_block = block[0].reshape(block_rows, head_count, HEAD)
        value_block = block[1].reshape(block_rows, head_count, HEAD)
        scores = (
            jnp.einsum("hqd,khd->hqk", queries, key_block, preferred_element_type=jnp.float32)
            * scale
        )
        key_pos = key_first + jnp.arange(block_rows, dtype=jnp.int32)
        allowed = (key_pos[None, :] >= starts[:, None]) & (key_pos[None, :] <= positions[:, None])
        scores = jnp.where(allowed[None], scores, MASKED)
        new_peak = jnp.maximum(peak, jnp.max(scores, axis=2))
        weights = jnp.where(allowed[None], jnp.exp(scores - new_peak[:, :, None]), 0.0)
        factor = jnp.exp(peak - new_peak)
        new_total = total * factor + jnp.sum(weights, axis=2)
        new_summed = summed * factor[:, :, None] + jnp.einsum(
            "hqk,khd->hqd",
            weights.astype(jnp.bfloat16),
            value_block,
            preferred_element_type=jnp.float32,
        )
        return (new_peak, new_total, new_summed)

    initial = (
        jnp.full((head_count, row_count), MASKED, jnp.float32),
        jnp.zeros((head_count, row_count), jnp.float32),
        jnp.zeros((head_count, row_count, HEAD), jnp.float32),
    )
    state = attend(initial, key_value, req_index * row_count)
    for shift in range(1, window + 1):
        pairs = [(i, i + shift) for i in range(req_count - shift)]
        block = lax.ppermute(key_value, "req", pairs)
        state = attend(state, block, (req_index - shift) * row_count)
    peak, total, summed = state
    attended = (summed / total[:, :, None]).astype(jnp.bfloat16)
    return jnp.transpose(attended, (1, 0, 2)).reshape(row_count, head_count * HEAD)


def solution(mesh):
    in_specs = (
        P("req", "tp"),
        P(),
        P(None, "tp"),
        P(None, "tp"),
        P(None, "tp"),
        P(),
        P(),
        P(None, "tp"),
        P(None, "tp"),
        P(),
        P(),
    )
    out_specs = P("req", "tp")
    fn = functools.partial(body, mesh.shape["req"])
    return jax.shard_map(fn, mesh=mesh, in_specs=in_specs, out_specs=out_specs, check_vma=False)
```

```python
import functools
import math

import jax
import jax.numpy as jnp
from jax import lax
from jax.sharding import PartitionSpec as P

HEAD = 128
ADAPTER_RANK = 16
ADAPTER_COUNT = 32


EPS = 1e-05
ADAPTER_SCALE = 0.5
MASKED = -1e30


def prompt_layout(lengths, positions):
    ends = jnp.cumsum(lengths)
    before = (ends[None, :] <= positions[:, None]).astype(jnp.int32)
    starts = jnp.sum(before * lengths[None, :], axis=1)
    prompt = jnp.sum(before, axis=1)
    return (starts, prompt)


def adapter_mask(prompt, prompt_adapter_index, count, rank):
    chosen = (
        prompt[:, None] == jnp.arange(prompt_adapter_index.shape[0], dtype=jnp.int32)[None, :]
    ).astype(jnp.int32)
    adapter = jnp.sum(chosen * prompt_adapter_index[None, :], axis=1)
    column = jnp.arange(count * rank, dtype=jnp.int32) // rank
    return (column[None, :] == adapter[:, None]).astype(jnp.float32)


def rotate(field, offsets, width):
    half = width // 2
    freq = jnp.exp(jnp.arange(half, dtype=jnp.float32) * (-2.0 * math.log(10000.0) / width))
    angle = offsets.astype(jnp.float32)[:, None] * freq[None, :]
    cosine = jnp.cos(angle)[:, None, :]
    sine = jnp.sin(angle)[:, None, :]
    first = field[..., :half]
    second = field[..., half:]
    return jnp.concatenate(
        [first * cosine - second * sine, second * cosine + first * sine], axis=-1
    )


MAXLEN = 8448


def body(
    req_count,
    tokens,
    input_norm_gain,
    query_weight,
    key_weight,
    value_weight,
    query_down_maps,
    value_down_maps,
    query_up_maps,
    value_up_maps,
    lengths,
    prompt_adapter_index,
):
    row_count = tokens.shape[0]
    req_index = lax.axis_index("req")
    positions = req_index * row_count + jnp.arange(row_count, dtype=jnp.int32)
    starts, prompt = prompt_layout(lengths, positions)
    causal_mask = adapter_mask(prompt, prompt_adapter_index, ADAPTER_COUNT, ADAPTER_RANK)
    incoming_weights = (query_weight, key_weight, value_weight, query_down_maps, value_down_maps)
    whole = lax.all_gather(tokens, "tp", axis=1, tiled=True)
    whole_float = whole.astype(jnp.float32)
    normed = (
        whole_float
        * lax.rsqrt(jnp.mean(whole_float * whole_float, axis=1, keepdims=True) + EPS)
        * input_norm_gain[None, :]
    ).astype(jnp.bfloat16)
    projected = tuple(
        (jnp.dot(normed, weight, preferred_element_type=jnp.float32) for weight in incoming_weights)
    )
    query_linear, key_lin, value_linear, query_middle, value_middle = projected
    query_middle = (query_middle * causal_mask).astype(jnp.bfloat16)
    value_middle = (value_middle * causal_mask).astype(jnp.bfloat16)
    query_linear = query_linear + ADAPTER_SCALE * jnp.dot(
        query_middle, query_up_maps, preferred_element_type=jnp.float32
    )
    value_rows = (
        value_linear
        + ADAPTER_SCALE * jnp.dot(value_middle, value_up_maps, preferred_element_type=jnp.float32)
    ).astype(jnp.bfloat16)
    head_count = query_linear.shape[1] // HEAD
    offsets = positions - starts
    queries = rotate(query_linear.reshape(row_count, head_count, HEAD), offsets, HEAD).astype(
        jnp.bfloat16
    )
    keys = rotate(key_lin.reshape(row_count, head_count, HEAD), offsets, HEAD).astype(jnp.bfloat16)
    values = value_rows.reshape(row_count, head_count, HEAD)
    scale = 1.0 / math.sqrt(HEAD)

    group = head_count
    span = group * row_count
    member = req_index % group
    chunk = req_index // group

    def group_pairs(step):
        return [
            (b * group + i, b * group + (i + step) % group)
            for b in range(req_count // group)
            for i in range(group)
        ]

    def regroup(parts, axis):
        order = (member - jnp.arange(group, dtype=jnp.int32)) % group
        return jnp.take(jnp.stack(parts), order, axis=axis)

    qkv = jnp.stack([queries, keys, values])
    parts = [lax.dynamic_index_in_dim(qkv, member, axis=2, keepdims=False)]
    for step in range(1, group):
        sent = lax.dynamic_index_in_dim(qkv, (member + step) % group, axis=2, keepdims=False)
        parts.append(lax.ppermute(sent, "req", group_pairs(step)))
    local = regroup(parts, 0)
    local = jnp.transpose(local, (1, 0, 2, 3)).reshape(3, span, HEAD)
    query_span = local[0]
    key_value = local[1:]

    span_positions = chunk * span + jnp.arange(span, dtype=jnp.int32)
    span_starts, _ = prompt_layout(lengths, span_positions)

    def attend(state, block, key_first):
        peak, total, summed = state
        key_block, value_block = block[0], block[1]
        scores = (
            jnp.einsum("qd,kd->qk", query_span, key_block, preferred_element_type=jnp.float32)
            * scale
        )
        key_pos = key_first + jnp.arange(key_block.shape[0], dtype=jnp.int32)
        allowed = (key_pos[None, :] >= span_starts[:, None]) & (
            key_pos[None, :] <= span_positions[:, None]
        )
        scores = jnp.where(allowed, scores, MASKED)
        new_peak = jnp.maximum(peak, jnp.max(scores, axis=1))
        weights = jnp.where(allowed, jnp.exp(scores - new_peak[:, None]), 0.0)
        factor = jnp.exp(peak - new_peak)
        new_total = total * factor + jnp.sum(weights, axis=1)
        new_summed = summed * factor[:, None] + jnp.dot(
            weights.astype(jnp.bfloat16), value_block, preferred_element_type=jnp.float32
        )
        return (new_peak, new_total, new_summed)

    state = (
        jnp.full((span,), MASKED, jnp.float32),
        jnp.zeros((span,), jnp.float32),
        jnp.zeros((span, HEAD), jnp.float32),
    )
    state = attend(state, key_value, chunk * span)
    chunk_count = req_count // group
    reach = MAXLEN - 1
    for back in range(1, chunk_count):
        if (back - 1) * span >= reach:
            break
        rows = min(span, -(-(reach - (back - 1) * span) // 128) * 128)
        pairs = [(i, i + back * group) for i in range(req_count - back * group)]
        block = lax.ppermute(key_value[:, span - rows :], "req", pairs)
        state = attend(state, block, (chunk - back) * span + span - rows)
    peak, total, summed = state
    attended = (summed / total[:, None]).astype(jnp.bfloat16).reshape(group, row_count, HEAD)

    parts = [lax.dynamic_index_in_dim(attended, member, axis=0, keepdims=False)]
    for step in range(1, group):
        sent = lax.dynamic_index_in_dim(attended, (member + step) % group, axis=0, keepdims=False)
        parts.append(lax.ppermute(sent, "req", group_pairs(step)))
    out = regroup(parts, 0)
    return jnp.transpose(out, (1, 0, 2)).reshape(row_count, head_count * HEAD)


def solution(mesh):
    in_specs = (
        P("req", "tp"),
        P(),
        P(None, "tp"),
        P(None, "tp"),
        P(None, "tp"),
        P(),
        P(),
        P(None, "tp"),
        P(None, "tp"),
        P(),
        P(),
    )
    out_specs = P("req", "tp")
    fn = functools.partial(body, mesh.shape["req"])
    return jax.shard_map(fn, mesh=mesh, in_specs=in_specs, out_specs=out_specs, check_vma=False)
```

```python
import functools
import math

import jax
import jax.numpy as jnp
from jax import lax
from jax.experimental import pallas as pl
from jax.experimental.pallas import tpu as pltpu
from jax.sharding import PartitionSpec as P

HEAD = 128
ADAPTER_RANK = 16
ADAPTER_COUNT = 32


EPS = 1e-05
ADAPTER_SCALE = 0.5
MASKED = -1e30


def prompt_layout(lengths, positions):
    ends = jnp.cumsum(lengths)
    before = (ends[None, :] <= positions[:, None]).astype(jnp.int32)
    starts = jnp.sum(before * lengths[None, :], axis=1)
    prompt = jnp.sum(before, axis=1)
    return (starts, prompt)


def adapter_mask(prompt, prompt_adapter_index, count, rank):
    chosen = (
        prompt[:, None] == jnp.arange(prompt_adapter_index.shape[0], dtype=jnp.int32)[None, :]
    ).astype(jnp.int32)
    adapter = jnp.sum(chosen * prompt_adapter_index[None, :], axis=1)
    column = jnp.arange(count * rank, dtype=jnp.int32) // rank
    return (column[None, :] == adapter[:, None]).astype(jnp.float32)


def rotate(field, offsets, width):
    half = width // 2
    freq = jnp.exp(jnp.arange(half, dtype=jnp.float32) * (-2.0 * math.log(10000.0) / width))
    angle = offsets.astype(jnp.float32)[:, None] * freq[None, :]
    cosine = jnp.cos(angle)[:, None, :]
    sine = jnp.sin(angle)[:, None, :]
    first = field[..., :half]
    second = field[..., half:]
    return jnp.concatenate(
        [first * cosine - second * sine, second * cosine + first * sine], axis=-1
    )


MAXLEN = 8448

QUERY_TILE = 1024
KEY_TILE = 512


def flash_kernel(meta, q_ref, k_ref, v_ref, start_ref, o_ref, peak_ref, total_ref, acc_ref):
    i = pl.program_id(0)
    j = pl.program_id(1)
    lo = meta[2 + 2 * i]
    hi = meta[3 + 2 * i]

    @pl.when(j == 0)
    def _():
        peak_ref[...] = jnp.full(peak_ref.shape, MASKED, jnp.float32)
        total_ref[...] = jnp.zeros(total_ref.shape, jnp.float32)
        acc_ref[...] = jnp.zeros(acc_ref.shape, jnp.float32)

    @pl.when(lo + j <= hi)
    def _():
        block = lo + j
        scores = lax.dot_general(
            q_ref[...], k_ref[...], (((1,), (1,)), ((), ())), preferred_element_type=jnp.float32
        ) * (1.0 / math.sqrt(HEAD))
        q_pos = meta[0] + i * QUERY_TILE + lax.broadcasted_iota(jnp.int32, (QUERY_TILE, 1), 0)
        k_pos = meta[1] + block * KEY_TILE + lax.broadcasted_iota(jnp.int32, (1, KEY_TILE), 1)
        allowed = (k_pos >= start_ref[...]) & (k_pos <= q_pos)
        scores = jnp.where(allowed, scores, MASKED)
        peak = peak_ref[...]
        new_peak = jnp.maximum(peak, jnp.max(scores, axis=1, keepdims=True))
        weights = jnp.where(allowed, jnp.exp(scores - new_peak), 0.0)
        factor = jnp.exp(peak - new_peak)
        total_ref[...] = total_ref[...] * factor + jnp.sum(weights, axis=1, keepdims=True)
        acc_ref[...] = acc_ref[...] * factor + jnp.dot(
            weights.astype(jnp.bfloat16), v_ref[...], preferred_element_type=jnp.float32
        )
        peak_ref[...] = new_peak

    @pl.when(j == pl.num_programs(1) - 1)
    def _():
        o_ref[...] = (acc_ref[...] / total_ref[...]).astype(o_ref.dtype)


def flash_attention(queries, keys, values, query_first, key_base, lengths):
    query_rows = queries.shape[0]
    key_rows = keys.shape[0]
    q_tiles = query_rows // QUERY_TILE
    k_tiles = key_rows // KEY_TILE
    positions = query_first + jnp.arange(query_rows, dtype=jnp.int32)
    starts, _ = prompt_layout(lengths, positions)
    tile_first = starts[::QUERY_TILE]
    tile_last = positions[QUERY_TILE - 1 :: QUERY_TILE]
    lo = jnp.clip((tile_first - key_base) // KEY_TILE, 0, k_tiles - 1)
    hi = jnp.clip((tile_last - key_base) // KEY_TILE, 0, k_tiles - 1)
    meta = jnp.concatenate(
        [jnp.stack([query_first, key_base]).astype(jnp.int32), jnp.stack([lo, hi], 1).reshape(-1)]
    ).astype(jnp.int32)

    def key_map(i, j, meta):
        return (jnp.minimum(meta[2 + 2 * i] + j, meta[3 + 2 * i]), 0)

    grid_spec = pltpu.PrefetchScalarGridSpec(
        num_scalar_prefetch=1,
        grid=(q_tiles, k_tiles),
        in_specs=[
            pl.BlockSpec((QUERY_TILE, HEAD), lambda i, j, meta: (i, 0)),
            pl.BlockSpec((KEY_TILE, HEAD), key_map),
            pl.BlockSpec((KEY_TILE, HEAD), key_map),
            pl.BlockSpec((QUERY_TILE, 1), lambda i, j, meta: (i, 0)),
        ],
        out_specs=pl.BlockSpec((QUERY_TILE, HEAD), lambda i, j, meta: (i, 0)),
        scratch_shapes=[
            pltpu.VMEM((QUERY_TILE, 1), jnp.float32),
            pltpu.VMEM((QUERY_TILE, 1), jnp.float32),
            pltpu.VMEM((QUERY_TILE, HEAD), jnp.float32),
        ],
    )
    return pl.pallas_call(
        flash_kernel,
        grid_spec=grid_spec,
        out_shape=jax.ShapeDtypeStruct((query_rows, HEAD), jnp.bfloat16),
        compiler_params=pltpu.CompilerParams(
            dimension_semantics=("arbitrary", "arbitrary"), vmem_limit_bytes=48 * 1024 * 1024
        ),
    )(meta, queries, keys, values, starts.reshape(query_rows, 1))


def body(
    req_count,
    tokens,
    input_norm_gain,
    query_weight,
    key_weight,
    value_weight,
    query_down_maps,
    value_down_maps,
    query_up_maps,
    value_up_maps,
    lengths,
    prompt_adapter_index,
):
    row_count = tokens.shape[0]
    req_index = lax.axis_index("req")
    positions = req_index * row_count + jnp.arange(row_count, dtype=jnp.int32)
    starts, prompt = prompt_layout(lengths, positions)
    causal_mask = adapter_mask(prompt, prompt_adapter_index, ADAPTER_COUNT, ADAPTER_RANK)
    incoming_weights = (query_weight, key_weight, value_weight, query_down_maps, value_down_maps)
    whole = lax.all_gather(tokens, "tp", axis=1, tiled=True)
    whole_float = whole.astype(jnp.float32)
    normed = (
        whole_float
        * lax.rsqrt(jnp.mean(whole_float * whole_float, axis=1, keepdims=True) + EPS)
        * input_norm_gain[None, :]
    ).astype(jnp.bfloat16)
    projected = tuple(
        (jnp.dot(normed, weight, preferred_element_type=jnp.float32) for weight in incoming_weights)
    )
    query_linear, key_lin, value_linear, query_middle, value_middle = projected
    query_middle = (query_middle * causal_mask).astype(jnp.bfloat16)
    value_middle = (value_middle * causal_mask).astype(jnp.bfloat16)
    query_linear = query_linear + ADAPTER_SCALE * jnp.dot(
        query_middle, query_up_maps, preferred_element_type=jnp.float32
    )
    value_rows = (
        value_linear
        + ADAPTER_SCALE * jnp.dot(value_middle, value_up_maps, preferred_element_type=jnp.float32)
    ).astype(jnp.bfloat16)
    head_count = query_linear.shape[1] // HEAD
    offsets = positions - starts
    queries = rotate(query_linear.reshape(row_count, head_count, HEAD), offsets, HEAD).astype(
        jnp.bfloat16
    )
    keys = rotate(key_lin.reshape(row_count, head_count, HEAD), offsets, HEAD).astype(jnp.bfloat16)
    values = value_rows.reshape(row_count, head_count, HEAD)
    scale = 1.0 / math.sqrt(HEAD)

    group = head_count
    span = group * row_count
    member = req_index % group
    chunk = req_index // group

    def group_pairs(step):
        return [
            (b * group + i, b * group + (i + step) % group)
            for b in range(req_count // group)
            for i in range(group)
        ]

    def regroup(parts, axis):
        order = (member - jnp.arange(group, dtype=jnp.int32)) % group
        return jnp.take(jnp.stack(parts), order, axis=axis)

    qkv = jnp.stack([queries, keys, values])
    parts = [lax.dynamic_index_in_dim(qkv, member, axis=2, keepdims=False)]
    for step in range(1, group):
        sent = lax.dynamic_index_in_dim(qkv, (member + step) % group, axis=2, keepdims=False)
        parts.append(lax.ppermute(sent, "req", group_pairs(step)))
    local = regroup(parts, 0)
    local = jnp.transpose(local, (1, 0, 2, 3)).reshape(3, span, HEAD)
    query_span = local[0]
    key_value = local[1:]

    chunk_count = req_count // group
    reach = MAXLEN - 1
    segments = [key_value]
    for back in range(1, chunk_count):
        if (back - 1) * span >= reach:
            break
        rows = min(span, -(-(reach - (back - 1) * span) // KEY_TILE) * KEY_TILE)
        pairs = [(i, i + back * group) for i in range(req_count - back * group)]
        segments.insert(0, lax.ppermute(key_value[:, span - rows :], "req", pairs))
    window = jnp.concatenate(segments, axis=1)
    key_base = chunk * span + span - window.shape[1]
    attended = flash_attention(query_span, window[0], window[1], chunk * span, key_base, lengths)
    attended = attended.reshape(group, row_count, HEAD)

    parts = [lax.dynamic_index_in_dim(attended, member, axis=0, keepdims=False)]
    for step in range(1, group):
        sent = lax.dynamic_index_in_dim(attended, (member + step) % group, axis=0, keepdims=False)
        parts.append(lax.ppermute(sent, "req", group_pairs(step)))
    out = regroup(parts, 0)
    return jnp.transpose(out, (1, 0, 2)).reshape(row_count, head_count * HEAD)


def solution(mesh):
    in_specs = (
        P("req", "tp"),
        P(),
        P(None, "tp"),
        P(None, "tp"),
        P(None, "tp"),
        P(),
        P(),
        P(None, "tp"),
        P(None, "tp"),
        P(),
        P(),
    )
    out_specs = P("req", "tp")
    fn = functools.partial(body, mesh.shape["req"])
    return jax.shard_map(fn, mesh=mesh, in_specs=in_specs, out_specs=out_specs, check_vma=False)
```

```python
import functools
import math

import jax
import jax.numpy as jnp
from jax import lax
from jax.experimental import pallas as pl
from jax.experimental.pallas import tpu as pltpu
from jax.sharding import PartitionSpec as P

HEAD = 128
ADAPTER_RANK = 16
ADAPTER_COUNT = 32


EPS = 1e-05
ADAPTER_SCALE = 0.5
MASKED = -1e30


def prompt_layout(lengths, positions):
    ends = jnp.cumsum(lengths)
    before = (ends[None, :] <= positions[:, None]).astype(jnp.int32)
    starts = jnp.sum(before * lengths[None, :], axis=1)
    prompt = jnp.sum(before, axis=1)
    return (starts, prompt)


def adapter_mask(prompt, prompt_adapter_index, count, rank):
    chosen = (
        prompt[:, None] == jnp.arange(prompt_adapter_index.shape[0], dtype=jnp.int32)[None, :]
    ).astype(jnp.int32)
    adapter = jnp.sum(chosen * prompt_adapter_index[None, :], axis=1)
    column = jnp.arange(count * rank, dtype=jnp.int32) // rank
    return (column[None, :] == adapter[:, None]).astype(jnp.float32)


def rotate(field, offsets, width):
    half = width // 2
    freq = jnp.exp(jnp.arange(half, dtype=jnp.float32) * (-2.0 * math.log(10000.0) / width))
    angle = offsets.astype(jnp.float32)[:, None] * freq[None, :]
    cosine = jnp.cos(angle)[:, None, :]
    sine = jnp.sin(angle)[:, None, :]
    first = field[..., :half]
    second = field[..., half:]
    return jnp.concatenate(
        [first * cosine - second * sine, second * cosine + first * sine], axis=-1
    )


MAXLEN = 8448

QUERY_TILE = 1024
KEY_TILE = 512


def flash_kernel(
    meta, q_ref, k_ref, v_ref, start_ref, peak_in, total_in, acc_in, peak_ref, total_ref, acc_ref
):
    i = pl.program_id(0)
    j = pl.program_id(1)
    lo = meta[2 + 2 * i]
    hi = meta[3 + 2 * i]

    @pl.when(j == 0)
    def _():
        peak_ref[...] = peak_in[...]
        total_ref[...] = total_in[...]
        acc_ref[...] = acc_in[...]

    @pl.when(lo + j <= hi)
    def _():
        block = lo + j
        scores = lax.dot_general(
            q_ref[...], k_ref[...], (((1,), (1,)), ((), ())), preferred_element_type=jnp.float32
        ) * (1.0 / math.sqrt(HEAD))
        q_pos = meta[0] + i * QUERY_TILE + lax.broadcasted_iota(jnp.int32, (QUERY_TILE, 1), 0)
        k_pos = meta[1] + block * KEY_TILE + lax.broadcasted_iota(jnp.int32, (1, KEY_TILE), 1)
        allowed = (k_pos >= start_ref[...]) & (k_pos <= q_pos)
        scores = jnp.where(allowed, scores, MASKED)
        peak = peak_ref[...]
        new_peak = jnp.maximum(peak, jnp.max(scores, axis=1, keepdims=True))
        weights = jnp.where(allowed, jnp.exp(scores - new_peak), 0.0)
        factor = jnp.exp(peak - new_peak)
        total_ref[...] = total_ref[...] * factor + jnp.sum(weights, axis=1, keepdims=True)
        acc_ref[...] = acc_ref[...] * factor + jnp.dot(
            weights.astype(jnp.bfloat16), v_ref[...], preferred_element_type=jnp.float32
        )
        peak_ref[...] = new_peak


def flash_step(state, queries, starts, key_value, query_first, key_base):
    query_rows = queries.shape[0]
    key_rows = key_value.shape[1]
    q_tiles = query_rows // QUERY_TILE
    k_tiles = key_rows // KEY_TILE
    positions = query_first + jnp.arange(query_rows, dtype=jnp.int32)
    tile_first = starts[::QUERY_TILE, 0]
    tile_last = positions[QUERY_TILE - 1 :: QUERY_TILE]
    lo = jnp.maximum((tile_first - key_base) // KEY_TILE, 0)
    hi = jnp.minimum((tile_last - key_base) // KEY_TILE, k_tiles - 1)
    meta = jnp.concatenate(
        [jnp.stack([query_first, key_base]).astype(jnp.int32), jnp.stack([lo, hi], 1).reshape(-1)]
    ).astype(jnp.int32)

    def key_map(i, j, meta):
        block = jnp.minimum(meta[2 + 2 * i] + j, meta[3 + 2 * i])
        return (0, jnp.clip(block, 0, k_tiles - 1), 0)

    row_spec = pl.BlockSpec((QUERY_TILE, 1), lambda i, j, meta: (i, 0))
    acc_spec = pl.BlockSpec((QUERY_TILE, HEAD), lambda i, j, meta: (i, 0))
    grid_spec = pltpu.PrefetchScalarGridSpec(
        num_scalar_prefetch=1,
        grid=(q_tiles, k_tiles),
        in_specs=[
            pl.BlockSpec((QUERY_TILE, HEAD), lambda i, j, meta: (i, 0)),
            pl.BlockSpec((None, KEY_TILE, HEAD), key_map),
            pl.BlockSpec((None, KEY_TILE, HEAD), lambda i, j, meta: (1,) + key_map(i, j, meta)[1:]),
            row_spec,
            row_spec,
            row_spec,
            acc_spec,
        ],
        out_specs=[row_spec, row_spec, acc_spec],
    )
    return pl.pallas_call(
        flash_kernel,
        grid_spec=grid_spec,
        out_shape=[jax.ShapeDtypeStruct(s.shape, jnp.float32) for s in state],
        input_output_aliases={5: 0, 6: 1, 7: 2},
        compiler_params=pltpu.CompilerParams(
            dimension_semantics=("arbitrary", "arbitrary"), vmem_limit_bytes=48 * 1024 * 1024
        ),
    )(meta, queries, key_value, key_value, starts, *state)


def body(
    req_count,
    tokens,
    input_norm_gain,
    query_weight,
    key_weight,
    value_weight,
    query_down_maps,
    value_down_maps,
    query_up_maps,
    value_up_maps,
    lengths,
    prompt_adapter_index,
):
    row_count = tokens.shape[0]
    req_index = lax.axis_index("req")
    positions = req_index * row_count + jnp.arange(row_count, dtype=jnp.int32)
    starts, prompt = prompt_layout(lengths, positions)
    causal_mask = adapter_mask(prompt, prompt_adapter_index, ADAPTER_COUNT, ADAPTER_RANK)
    incoming_weights = (query_weight, key_weight, value_weight, query_down_maps, value_down_maps)
    whole = lax.all_gather(tokens, "tp", axis=1, tiled=True)
    whole_float = whole.astype(jnp.float32)
    normed = (
        whole_float
        * lax.rsqrt(jnp.mean(whole_float * whole_float, axis=1, keepdims=True) + EPS)
        * input_norm_gain[None, :]
    ).astype(jnp.bfloat16)
    projected = tuple(
        (jnp.dot(normed, weight, preferred_element_type=jnp.float32) for weight in incoming_weights)
    )
    query_linear, key_lin, value_linear, query_middle, value_middle = projected
    query_middle = (query_middle * causal_mask).astype(jnp.bfloat16)
    value_middle = (value_middle * causal_mask).astype(jnp.bfloat16)
    query_linear = query_linear + ADAPTER_SCALE * jnp.dot(
        query_middle, query_up_maps, preferred_element_type=jnp.float32
    )
    value_rows = (
        value_linear
        + ADAPTER_SCALE * jnp.dot(value_middle, value_up_maps, preferred_element_type=jnp.float32)
    ).astype(jnp.bfloat16)
    head_count = query_linear.shape[1] // HEAD
    offsets = positions - starts
    queries = rotate(query_linear.reshape(row_count, head_count, HEAD), offsets, HEAD).astype(
        jnp.bfloat16
    )
    keys = rotate(key_lin.reshape(row_count, head_count, HEAD), offsets, HEAD).astype(jnp.bfloat16)
    values = value_rows.reshape(row_count, head_count, HEAD)
    scale = 1.0 / math.sqrt(HEAD)

    group = head_count
    span = group * row_count
    member = req_index % group
    chunk = req_index // group

    def group_pairs(step):
        return [
            (b * group + i, b * group + (i + step) % group)
            for b in range(req_count // group)
            for i in range(group)
        ]

    def regroup(parts, axis):
        order = (member - jnp.arange(group, dtype=jnp.int32)) % group
        return jnp.take(jnp.stack(parts), order, axis=axis)

    qkv = jnp.stack([queries, keys, values])
    parts = [lax.dynamic_index_in_dim(qkv, member, axis=2, keepdims=False)]
    for step in range(1, group):
        sent = lax.dynamic_index_in_dim(qkv, (member + step) % group, axis=2, keepdims=False)
        parts.append(lax.ppermute(sent, "req", group_pairs(step)))
    local = regroup(parts, 0)
    local = jnp.transpose(local, (1, 0, 2, 3)).reshape(3, span, HEAD)
    query_span = local[0]
    key_value = local[1:]

    chunk_count = req_count // group
    reach = MAXLEN - 1
    span_positions = chunk * span + jnp.arange(span, dtype=jnp.int32)
    span_starts, _ = prompt_layout(lengths, span_positions)
    span_starts = span_starts.reshape(span, 1)
    state = (
        jnp.full((span, 1), MASKED, jnp.float32),
        jnp.zeros((span, 1), jnp.float32),
        jnp.zeros((span, HEAD), jnp.float32),
    )
    arrived = [(key_value, chunk * span)]
    for back in range(1, chunk_count):
        if (back - 1) * span >= reach:
            break
        rows = min(span, -(-(reach - (back - 1) * span) // KEY_TILE) * KEY_TILE)
        pairs = [(i, i + back * group) for i in range(req_count - back * group)]
        segment = lax.ppermute(key_value[:, span - rows :], "req", pairs)
        arrived.append((segment, (chunk - back) * span + span - rows))
    for segment, key_base in arrived:
        state = flash_step(state, query_span, span_starts, segment, chunk * span, key_base)
    peak, total, summed = state
    attended = (summed / total).astype(jnp.bfloat16)
    attended = attended.reshape(group, row_count, HEAD)

    parts = [lax.dynamic_index_in_dim(attended, member, axis=0, keepdims=False)]
    for step in range(1, group):
        sent = lax.dynamic_index_in_dim(attended, (member + step) % group, axis=0, keepdims=False)
        parts.append(lax.ppermute(sent, "req", group_pairs(step)))
    out = regroup(parts, 0)
    return jnp.transpose(out, (1, 0, 2)).reshape(row_count, head_count * HEAD)


def solution(mesh):
    in_specs = (
        P("req", "tp"),
        P(),
        P(None, "tp"),
        P(None, "tp"),
        P(None, "tp"),
        P(),
        P(),
        P(None, "tp"),
        P(None, "tp"),
        P(),
        P(),
    )
    out_specs = P("req", "tp")
    fn = functools.partial(body, mesh.shape["req"])
    return jax.shard_map(fn, mesh=mesh, in_specs=in_specs, out_specs=out_specs, check_vma=False)
```

```python
import functools
import math

import jax
import jax.numpy as jnp
from jax import lax
from jax.experimental import pallas as pl
from jax.experimental.pallas import tpu as pltpu
from jax.sharding import PartitionSpec as P

HEAD = 128
ADAPTER_RANK = 16
ADAPTER_COUNT = 32


EPS = 1e-05
ADAPTER_SCALE = 0.5
MASKED = -1e30


def prompt_layout(lengths, positions):
    ends = jnp.cumsum(lengths)
    before = (ends[None, :] <= positions[:, None]).astype(jnp.int32)
    starts = jnp.sum(before * lengths[None, :], axis=1)
    prompt = jnp.sum(before, axis=1)
    return (starts, prompt)


def adapter_mask(prompt, prompt_adapter_index, count, rank):
    chosen = (
        prompt[:, None] == jnp.arange(prompt_adapter_index.shape[0], dtype=jnp.int32)[None, :]
    ).astype(jnp.int32)
    adapter = jnp.sum(chosen * prompt_adapter_index[None, :], axis=1)
    column = jnp.arange(count * rank, dtype=jnp.int32) // rank
    return (column[None, :] == adapter[:, None]).astype(jnp.float32)


def rotate(field, offsets, width):
    half = width // 2
    freq = jnp.exp(jnp.arange(half, dtype=jnp.float32) * (-2.0 * math.log(10000.0) / width))
    angle = offsets.astype(jnp.float32)[:, None] * freq[None, :]
    cosine = jnp.cos(angle)[:, None, :]
    sine = jnp.sin(angle)[:, None, :]
    first = field[..., :half]
    second = field[..., half:]
    return jnp.concatenate(
        [first * cosine - second * sine, second * cosine + first * sine], axis=-1
    )


MAXLEN = 8448

QUERY_TILE = 1024
KEY_TILE = 512


def flash_kernel(
    meta, q_ref, k_ref, v_ref, start_ref, peak_in, total_in, acc_in, peak_ref, total_ref, acc_ref
):
    i = pl.program_id(0)
    j = pl.program_id(1)
    lo = meta[2 + 2 * i]
    hi = meta[3 + 2 * i]

    @pl.when(j == 0)
    def _():
        peak_ref[...] = peak_in[...]
        total_ref[...] = total_in[...]
        acc_ref[...] = acc_in[...]

    @pl.when(lo + j <= hi)
    def _():
        block = lo + j
        scores = lax.dot_general(
            q_ref[...], k_ref[...], (((1,), (1,)), ((), ())), preferred_element_type=jnp.float32
        ) * (1.0 / math.sqrt(HEAD))
        q_pos = meta[0] + i * QUERY_TILE + lax.broadcasted_iota(jnp.int32, (QUERY_TILE, 1), 0)
        k_pos = meta[1] + block * KEY_TILE + lax.broadcasted_iota(jnp.int32, (1, KEY_TILE), 1)
        allowed = (k_pos >= start_ref[...]) & (k_pos <= q_pos)
        scores = jnp.where(allowed, scores, MASKED)
        peak = peak_ref[...]
        new_peak = jnp.maximum(peak, jnp.max(scores, axis=1, keepdims=True))
        weights = jnp.where(allowed, jnp.exp(scores - new_peak), 0.0)
        factor = jnp.exp(peak - new_peak)
        total_ref[...] = total_ref[...] * factor + jnp.sum(weights, axis=1, keepdims=True)
        acc_ref[...] = acc_ref[...] * factor + jnp.dot(
            weights.astype(jnp.bfloat16), v_ref[...], preferred_element_type=jnp.float32
        )
        peak_ref[...] = new_peak


def flash_step(state, queries, starts, key_value, query_first, key_base):
    query_rows = queries.shape[0]
    key_rows = key_value.shape[1]
    q_tiles = query_rows // QUERY_TILE
    k_tiles = key_rows // KEY_TILE
    positions = query_first + jnp.arange(query_rows, dtype=jnp.int32)
    tile_first = starts[::QUERY_TILE, 0]
    tile_last = positions[QUERY_TILE - 1 :: QUERY_TILE]
    lo = jnp.maximum((tile_first - key_base) // KEY_TILE, 0)
    hi = jnp.minimum((tile_last - key_base) // KEY_TILE, k_tiles - 1)
    meta = jnp.concatenate(
        [jnp.stack([query_first, key_base]).astype(jnp.int32), jnp.stack([lo, hi], 1).reshape(-1)]
    ).astype(jnp.int32)

    def key_map(i, j, meta):
        block = jnp.minimum(meta[2 + 2 * i] + j, meta[3 + 2 * i])
        return (0, jnp.clip(block, 0, k_tiles - 1), 0)

    row_spec = pl.BlockSpec((QUERY_TILE, 1), lambda i, j, meta: (i, 0))
    acc_spec = pl.BlockSpec((QUERY_TILE, HEAD), lambda i, j, meta: (i, 0))
    grid_spec = pltpu.PrefetchScalarGridSpec(
        num_scalar_prefetch=1,
        grid=(q_tiles, k_tiles),
        in_specs=[
            pl.BlockSpec((QUERY_TILE, HEAD), lambda i, j, meta: (i, 0)),
            pl.BlockSpec((None, KEY_TILE, HEAD), key_map),
            pl.BlockSpec((None, KEY_TILE, HEAD), lambda i, j, meta: (1,) + key_map(i, j, meta)[1:]),
            row_spec,
            row_spec,
            row_spec,
            acc_spec,
        ],
        out_specs=[row_spec, row_spec, acc_spec],
    )
    return pl.pallas_call(
        flash_kernel,
        grid_spec=grid_spec,
        out_shape=[jax.ShapeDtypeStruct(s.shape, jnp.float32) for s in state],
        input_output_aliases={5: 0, 6: 1, 7: 2},
        compiler_params=pltpu.CompilerParams(
            dimension_semantics=("arbitrary", "arbitrary"), vmem_limit_bytes=48 * 1024 * 1024
        ),
    )(meta, queries, key_value, key_value, starts, *state)


def body(
    req_count,
    tokens,
    input_norm_gain,
    query_weight,
    key_weight,
    value_weight,
    query_down_maps,
    value_down_maps,
    query_up_maps,
    value_up_maps,
    lengths,
    prompt_adapter_index,
):
    row_count = tokens.shape[0]
    req_index = lax.axis_index("req")
    positions = req_index * row_count + jnp.arange(row_count, dtype=jnp.int32)
    starts, prompt = prompt_layout(lengths, positions)
    causal_mask = adapter_mask(prompt, prompt_adapter_index, ADAPTER_COUNT, ADAPTER_RANK)
    incoming_weights = (query_weight, key_weight, value_weight, query_down_maps, value_down_maps)
    tp_count = input_norm_gain.shape[0] // tokens.shape[1]
    width = tokens.shape[1]
    tp_index = lax.axis_index("tp")
    own_float = tokens.astype(jnp.float32)
    square_sum = lax.psum(jnp.sum(own_float * own_float, axis=1, keepdims=True), "tp")
    inverse = lax.rsqrt(square_sum / input_norm_gain.shape[0] + EPS)
    chunks = [(tokens, tp_index)]
    for step in range(1, tp_count):
        pairs = [(i, (i - step) % tp_count) for i in range(tp_count)]
        chunks.append((lax.ppermute(tokens, "tp", pairs), (tp_index + step) % tp_count))
    projected = [None] * len(incoming_weights)
    for chunk, index in chunks:
        gain = lax.dynamic_slice_in_dim(input_norm_gain, index * width, width)
        normed = (chunk.astype(jnp.float32) * inverse * gain[None, :]).astype(jnp.bfloat16)
        for n, weight in enumerate(incoming_weights):
            rows = lax.dynamic_slice_in_dim(weight, index * width, width, axis=0)
            part = jnp.dot(normed, rows, preferred_element_type=jnp.float32)
            projected[n] = part if projected[n] is None else projected[n] + part
    query_linear, key_lin, value_linear, query_middle, value_middle = projected
    query_middle = (query_middle * causal_mask).astype(jnp.bfloat16)
    value_middle = (value_middle * causal_mask).astype(jnp.bfloat16)
    query_linear = query_linear + ADAPTER_SCALE * jnp.dot(
        query_middle, query_up_maps, preferred_element_type=jnp.float32
    )
    value_rows = (
        value_linear
        + ADAPTER_SCALE * jnp.dot(value_middle, value_up_maps, preferred_element_type=jnp.float32)
    ).astype(jnp.bfloat16)
    head_count = query_linear.shape[1] // HEAD
    offsets = positions - starts
    queries = rotate(query_linear.reshape(row_count, head_count, HEAD), offsets, HEAD).astype(
        jnp.bfloat16
    )
    keys = rotate(key_lin.reshape(row_count, head_count, HEAD), offsets, HEAD).astype(jnp.bfloat16)
    values = value_rows.reshape(row_count, head_count, HEAD)
    scale = 1.0 / math.sqrt(HEAD)

    group = head_count
    span = group * row_count
    member = req_index % group
    chunk = req_index // group

    def group_pairs(step):
        return [
            (b * group + i, b * group + (i + step) % group)
            for b in range(req_count // group)
            for i in range(group)
        ]

    def regroup(parts, axis):
        order = (member - jnp.arange(group, dtype=jnp.int32)) % group
        return jnp.take(jnp.stack(parts), order, axis=axis)

    qkv = jnp.stack([queries, keys, values])
    parts = [lax.dynamic_index_in_dim(qkv, member, axis=2, keepdims=False)]
    for step in range(1, group):
        sent = lax.dynamic_index_in_dim(qkv, (member + step) % group, axis=2, keepdims=False)
        parts.append(lax.ppermute(sent, "req", group_pairs(step)))
    local = regroup(parts, 0)
    local = jnp.transpose(local, (1, 0, 2, 3)).reshape(3, span, HEAD)
    query_span = local[0]
    key_value = local[1:]

    chunk_count = req_count // group
    reach = MAXLEN - 1
    span_positions = chunk * span + jnp.arange(span, dtype=jnp.int32)
    span_starts, _ = prompt_layout(lengths, span_positions)
    span_starts = span_starts.reshape(span, 1)
    state = (
        jnp.full((span, 1), MASKED, jnp.float32),
        jnp.zeros((span, 1), jnp.float32),
        jnp.zeros((span, HEAD), jnp.float32),
    )
    arrived = [(key_value, chunk * span)]
    for back in range(1, chunk_count):
        if (back - 1) * span >= reach:
            break
        rows = min(span, -(-(reach - (back - 1) * span) // KEY_TILE) * KEY_TILE)
        pairs = [(i, i + back * group) for i in range(req_count - back * group)]
        segment = lax.ppermute(key_value[:, span - rows :], "req", pairs)
        arrived.append((segment, (chunk - back) * span + span - rows))
    for segment, key_base in arrived:
        state = flash_step(state, query_span, span_starts, segment, chunk * span, key_base)
    peak, total, summed = state
    attended = (summed / total).astype(jnp.bfloat16)
    attended = attended.reshape(group, row_count, HEAD)

    parts = [lax.dynamic_index_in_dim(attended, member, axis=0, keepdims=False)]
    for step in range(1, group):
        sent = lax.dynamic_index_in_dim(attended, (member + step) % group, axis=0, keepdims=False)
        parts.append(lax.ppermute(sent, "req", group_pairs(step)))
    out = regroup(parts, 0)
    return jnp.transpose(out, (1, 0, 2)).reshape(row_count, head_count * HEAD)


def solution(mesh):
    in_specs = (
        P("req", "tp"),
        P(),
        P(None, "tp"),
        P(None, "tp"),
        P(None, "tp"),
        P(),
        P(),
        P(None, "tp"),
        P(None, "tp"),
        P(),
        P(),
    )
    out_specs = P("req", "tp")
    fn = functools.partial(body, mesh.shape["req"])
    return jax.shard_map(fn, mesh=mesh, in_specs=in_specs, out_specs=out_specs, check_vma=False)
```

```python
import functools
import math

import jax
import jax.numpy as jnp
from jax import lax
from jax.experimental import pallas as pl
from jax.experimental.pallas import tpu as pltpu
from jax.sharding import PartitionSpec as P

HEAD = 128
ADAPTER_RANK = 16
ADAPTER_COUNT = 32


EPS = 1e-05
ADAPTER_SCALE = 0.5
MASKED = -1e30


def prompt_layout(lengths, positions):
    ends = jnp.cumsum(lengths)
    before = (ends[None, :] <= positions[:, None]).astype(jnp.int32)
    starts = jnp.sum(before * lengths[None, :], axis=1)
    prompt = jnp.sum(before, axis=1)
    return (starts, prompt)


def adapter_mask(prompt, prompt_adapter_index, count, rank):
    chosen = (
        prompt[:, None] == jnp.arange(prompt_adapter_index.shape[0], dtype=jnp.int32)[None, :]
    ).astype(jnp.int32)
    adapter = jnp.sum(chosen * prompt_adapter_index[None, :], axis=1)
    column = jnp.arange(count * rank, dtype=jnp.int32) // rank
    return (column[None, :] == adapter[:, None]).astype(jnp.float32)


def rotate(field, offsets, width):
    half = width // 2
    freq = jnp.exp(jnp.arange(half, dtype=jnp.float32) * (-2.0 * math.log(10000.0) / width))
    angle = offsets.astype(jnp.float32)[:, None] * freq[None, :]
    cosine = jnp.cos(angle)[:, None, :]
    sine = jnp.sin(angle)[:, None, :]
    first = field[..., :half]
    second = field[..., half:]
    return jnp.concatenate(
        [first * cosine - second * sine, second * cosine + first * sine], axis=-1
    )


MAXLEN = 8448

QUERY_TILE = 1024
KEY_TILE = 512


def flash_kernel(
    meta, q_ref, k_ref, v_ref, start_ref, peak_in, total_in, acc_in, peak_ref, total_ref, acc_ref
):
    i = pl.program_id(0)
    j = pl.program_id(1)
    lo = meta[2 + 2 * i]
    hi = meta[3 + 2 * i]

    @pl.when(j == 0)
    def _():
        peak_ref[...] = peak_in[...]
        total_ref[...] = total_in[...]
        acc_ref[...] = acc_in[...]

    @pl.when(lo + j <= hi)
    def _():
        block = lo + j
        scores = lax.dot_general(
            q_ref[...], k_ref[...], (((1,), (1,)), ((), ())), preferred_element_type=jnp.float32
        ) * (1.0 / math.sqrt(HEAD))
        q_pos = meta[0] + i * QUERY_TILE + lax.broadcasted_iota(jnp.int32, (QUERY_TILE, 1), 0)
        k_pos = meta[1] + block * KEY_TILE + lax.broadcasted_iota(jnp.int32, (1, KEY_TILE), 1)
        allowed = (k_pos >= start_ref[...]) & (k_pos <= q_pos)
        scores = jnp.where(allowed, scores, MASKED)
        peak = peak_ref[...]
        new_peak = jnp.maximum(peak, jnp.max(scores, axis=1, keepdims=True))
        weights = jnp.where(allowed, jnp.exp(scores - new_peak), 0.0)
        factor = jnp.exp(peak - new_peak)
        total_ref[...] = total_ref[...] * factor + jnp.sum(weights, axis=1, keepdims=True)
        acc_ref[...] = acc_ref[...] * factor + jnp.dot(
            weights.astype(jnp.bfloat16), v_ref[...], preferred_element_type=jnp.float32
        )
        peak_ref[...] = new_peak


def flash_step(state, queries, starts, key_value, query_first, key_base):
    query_rows = queries.shape[0]
    key_rows = key_value.shape[1]
    q_tiles = query_rows // QUERY_TILE
    k_tiles = key_rows // KEY_TILE
    positions = query_first + jnp.arange(query_rows, dtype=jnp.int32)
    tile_first = starts[::QUERY_TILE, 0]
    tile_last = positions[QUERY_TILE - 1 :: QUERY_TILE]
    lo = jnp.maximum((tile_first - key_base) // KEY_TILE, 0)
    hi = jnp.minimum((tile_last - key_base) // KEY_TILE, k_tiles - 1)
    meta = jnp.concatenate(
        [jnp.stack([query_first, key_base]).astype(jnp.int32), jnp.stack([lo, hi], 1).reshape(-1)]
    ).astype(jnp.int32)

    def key_map(i, j, meta):
        block = jnp.minimum(meta[2 + 2 * i] + j, meta[3 + 2 * i])
        return (0, jnp.clip(block, 0, k_tiles - 1), 0)

    row_spec = pl.BlockSpec((QUERY_TILE, 1), lambda i, j, meta: (i, 0))
    acc_spec = pl.BlockSpec((QUERY_TILE, HEAD), lambda i, j, meta: (i, 0))
    grid_spec = pltpu.PrefetchScalarGridSpec(
        num_scalar_prefetch=1,
        grid=(q_tiles, k_tiles),
        in_specs=[
            pl.BlockSpec((QUERY_TILE, HEAD), lambda i, j, meta: (i, 0)),
            pl.BlockSpec((None, KEY_TILE, HEAD), key_map),
            pl.BlockSpec((None, KEY_TILE, HEAD), lambda i, j, meta: (1,) + key_map(i, j, meta)[1:]),
            row_spec,
            row_spec,
            row_spec,
            acc_spec,
        ],
        out_specs=[row_spec, row_spec, acc_spec],
    )
    return pl.pallas_call(
        flash_kernel,
        grid_spec=grid_spec,
        out_shape=[jax.ShapeDtypeStruct(s.shape, jnp.float32) for s in state],
        input_output_aliases={5: 0, 6: 1, 7: 2},
        compiler_params=pltpu.CompilerParams(
            dimension_semantics=("arbitrary", "arbitrary"), vmem_limit_bytes=48 * 1024 * 1024
        ),
    )(meta, queries, key_value, key_value, starts, *state)


def body(
    req_count,
    tokens,
    input_norm_gain,
    query_weight,
    key_weight,
    value_weight,
    query_down_maps,
    value_down_maps,
    query_up_maps,
    value_up_maps,
    lengths,
    prompt_adapter_index,
):
    row_count = tokens.shape[0]
    req_index = lax.axis_index("req")
    positions = req_index * row_count + jnp.arange(row_count, dtype=jnp.int32)
    starts, prompt = prompt_layout(lengths, positions)
    causal_mask = adapter_mask(prompt, prompt_adapter_index, ADAPTER_COUNT, ADAPTER_RANK)
    incoming_weights = (query_weight, key_weight, value_weight, query_down_maps, value_down_maps)
    whole = lax.all_gather(tokens, "tp", axis=1, tiled=True)
    whole_float = whole.astype(jnp.float32)
    normed = (
        whole_float
        * lax.rsqrt(jnp.mean(whole_float * whole_float, axis=1, keepdims=True) + EPS)
        * input_norm_gain[None, :]
    ).astype(jnp.bfloat16)
    projected = tuple(
        (jnp.dot(normed, weight, preferred_element_type=jnp.float32) for weight in incoming_weights)
    )
    query_linear, key_lin, value_linear, query_middle, value_middle = projected
    query_middle = (query_middle * causal_mask).astype(jnp.bfloat16)
    value_middle = (value_middle * causal_mask).astype(jnp.bfloat16)
    query_linear = query_linear + ADAPTER_SCALE * jnp.dot(
        query_middle, query_up_maps, preferred_element_type=jnp.float32
    )
    value_rows = (
        value_linear
        + ADAPTER_SCALE * jnp.dot(value_middle, value_up_maps, preferred_element_type=jnp.float32)
    ).astype(jnp.bfloat16)
    head_count = query_linear.shape[1] // HEAD
    offsets = positions - starts
    queries = rotate(query_linear.reshape(row_count, head_count, HEAD), offsets, HEAD).astype(
        jnp.bfloat16
    )
    keys = rotate(key_lin.reshape(row_count, head_count, HEAD), offsets, HEAD).astype(jnp.bfloat16)
    values = value_rows.reshape(row_count, head_count, HEAD)
    scale = 1.0 / math.sqrt(HEAD)

    group = head_count
    span = group * row_count
    member = req_index % group
    chunk = req_index // group

    def group_pairs(step):
        return [
            (b * group + i, b * group + (i + step) % group)
            for b in range(req_count // group)
            for i in range(group)
        ]

    def regroup(parts, axis):
        order = (member - jnp.arange(group, dtype=jnp.int32)) % group
        return jnp.take(jnp.stack(parts), order, axis=axis)

    kv_rows = jnp.stack([keys, values])
    qkv = jnp.stack([queries, keys, values])
    parts = [lax.dynamic_index_in_dim(qkv, member, axis=2, keepdims=False)]
    for step in range(1, group):
        sent = lax.dynamic_index_in_dim(qkv, (member + step) % group, axis=2, keepdims=False)
        parts.append(lax.ppermute(sent, "req", group_pairs(step)))
    local = regroup(parts, 0)
    local = jnp.transpose(local, (1, 0, 2, 3)).reshape(3, span, HEAD)
    query_span = local[0]
    key_value = local[1:]

    chunk_count = req_count // group
    reach = MAXLEN - 1
    span_positions = chunk * span + jnp.arange(span, dtype=jnp.int32)
    span_starts, _ = prompt_layout(lengths, span_positions)
    span_starts = span_starts.reshape(span, 1)
    state = (
        jnp.full((span, 1), MASKED, jnp.float32),
        jnp.zeros((span, 1), jnp.float32),
        jnp.zeros((span, HEAD), jnp.float32),
    )
    arrived = [(key_value, chunk * span)]
    for back in range(1, chunk_count):
        if (back - 1) * span >= reach:
            break
        tile = max(KEY_TILE, row_count)
        rows = min(span, -(-(reach - (back - 1) * span) // tile) * tile)
        first = group - rows // row_count
        parts = []
        for step in range(group):
            pairs = [
                ((b - back) * group + p, b * group + (p + step) % group)
                for b in range(back, chunk_count)
                for p in range(first, group)
            ]
            sent = lax.dynamic_index_in_dim(
                kv_rows, (member + step) % group, axis=2, keepdims=False
            )
            parts.append(lax.ppermute(sent, "req", pairs))
        order = (member - jnp.arange(first, group, dtype=jnp.int32)) % group
        segment = jnp.take(jnp.stack(parts), order, axis=0)
        segment = jnp.transpose(segment, (1, 0, 2, 3)).reshape(2, rows, HEAD)
        arrived.append((segment, (chunk - back) * span + span - rows))
    for segment, key_base in arrived:
        state = flash_step(state, query_span, span_starts, segment, chunk * span, key_base)
    peak, total, summed = state
    attended = (summed / total).astype(jnp.bfloat16)
    attended = attended.reshape(group, row_count, HEAD)

    parts = [lax.dynamic_index_in_dim(attended, member, axis=0, keepdims=False)]
    for step in range(1, group):
        sent = lax.dynamic_index_in_dim(attended, (member + step) % group, axis=0, keepdims=False)
        parts.append(lax.ppermute(sent, "req", group_pairs(step)))
    out = regroup(parts, 0)
    return jnp.transpose(out, (1, 0, 2)).reshape(row_count, head_count * HEAD)


def solution(mesh):
    in_specs = (
        P("req", "tp"),
        P(),
        P(None, "tp"),
        P(None, "tp"),
        P(None, "tp"),
        P(),
        P(),
        P(None, "tp"),
        P(None, "tp"),
        P(),
        P(),
    )
    out_specs = P("req", "tp")
    fn = functools.partial(body, mesh.shape["req"])
    return jax.shard_map(fn, mesh=mesh, in_specs=in_specs, out_specs=out_specs, check_vma=False)
```

```python
import functools
import math

import jax
import jax.numpy as jnp
from jax import lax
from jax.experimental import pallas as pl
from jax.experimental.pallas import tpu as pltpu
from jax.sharding import PartitionSpec as P

HEAD = 128
ADAPTER_RANK = 16
ADAPTER_COUNT = 32


EPS = 1e-05
ADAPTER_SCALE = 0.5
MASKED = -1e30


def prompt_layout(lengths, positions):
    ends = jnp.cumsum(lengths)
    before = (ends[None, :] <= positions[:, None]).astype(jnp.int32)
    starts = jnp.sum(before * lengths[None, :], axis=1)
    prompt = jnp.sum(before, axis=1)
    return (starts, prompt)


def adapter_mask(prompt, prompt_adapter_index, count, rank):
    chosen = (
        prompt[:, None] == jnp.arange(prompt_adapter_index.shape[0], dtype=jnp.int32)[None, :]
    ).astype(jnp.int32)
    adapter = jnp.sum(chosen * prompt_adapter_index[None, :], axis=1)
    column = jnp.arange(count * rank, dtype=jnp.int32) // rank
    return (column[None, :] == adapter[:, None]).astype(jnp.float32)


def rotate(field, offsets, width):
    half = width // 2
    freq = jnp.exp(jnp.arange(half, dtype=jnp.float32) * (-2.0 * math.log(10000.0) / width))
    angle = offsets.astype(jnp.float32)[:, None] * freq[None, :]
    cosine = jnp.cos(angle)[:, None, :]
    sine = jnp.sin(angle)[:, None, :]
    first = field[..., :half]
    second = field[..., half:]
    return jnp.concatenate(
        [first * cosine - second * sine, second * cosine + first * sine], axis=-1
    )


MAXLEN = 8448

QUERY_TILE = 1024
KEY_TILE = 512


def flash_kernel(
    meta, q_ref, k_ref, v_ref, start_ref, peak_in, total_in, acc_in, peak_ref, total_ref, acc_ref
):
    i = pl.program_id(0)
    j = pl.program_id(1)
    lo = meta[2 + 2 * i]
    hi = meta[3 + 2 * i]

    @pl.when(j == 0)
    def _():
        peak_ref[...] = peak_in[...]
        total_ref[...] = total_in[...]
        acc_ref[...] = acc_in[...]

    @pl.when(lo + j <= hi)
    def _():
        block = lo + j
        scores = lax.dot_general(
            q_ref[...], k_ref[...], (((1,), (1,)), ((), ())), preferred_element_type=jnp.float32
        ) * (1.0 / math.sqrt(HEAD))
        q_pos = meta[0] + i * QUERY_TILE + lax.broadcasted_iota(jnp.int32, (QUERY_TILE, 1), 0)
        k_pos = meta[1] + block * KEY_TILE + lax.broadcasted_iota(jnp.int32, (1, KEY_TILE), 1)
        allowed = (k_pos >= start_ref[...]) & (k_pos <= q_pos)
        scores = jnp.where(allowed, scores, MASKED)
        peak = peak_ref[...]
        new_peak = jnp.maximum(peak, jnp.max(scores, axis=1, keepdims=True))
        weights = jnp.where(allowed, jnp.exp(scores - new_peak), 0.0)
        factor = jnp.exp(peak - new_peak)
        total_ref[...] = total_ref[...] * factor + jnp.sum(weights, axis=1, keepdims=True)
        acc_ref[...] = acc_ref[...] * factor + jnp.dot(
            weights.astype(jnp.bfloat16), v_ref[...], preferred_element_type=jnp.float32
        )
        peak_ref[...] = new_peak


def flash_step(state, queries, starts, key_value, query_first, key_base):
    query_rows = queries.shape[0]
    key_rows = key_value.shape[1]
    q_tiles = query_rows // QUERY_TILE
    k_tiles = key_rows // KEY_TILE
    positions = query_first + jnp.arange(query_rows, dtype=jnp.int32)
    tile_first = starts[::QUERY_TILE, 0]
    tile_last = positions[QUERY_TILE - 1 :: QUERY_TILE]
    lo = jnp.maximum((tile_first - key_base) // KEY_TILE, 0)
    hi = jnp.minimum((tile_last - key_base) // KEY_TILE, k_tiles - 1)
    meta = jnp.concatenate(
        [jnp.stack([query_first, key_base]).astype(jnp.int32), jnp.stack([lo, hi], 1).reshape(-1)]
    ).astype(jnp.int32)

    def key_map(i, j, meta):
        block = jnp.minimum(meta[2 + 2 * i] + j, meta[3 + 2 * i])
        return (0, jnp.clip(block, 0, k_tiles - 1), 0)

    row_spec = pl.BlockSpec((QUERY_TILE, 1), lambda i, j, meta: (i, 0))
    acc_spec = pl.BlockSpec((QUERY_TILE, HEAD), lambda i, j, meta: (i, 0))
    grid_spec = pltpu.PrefetchScalarGridSpec(
        num_scalar_prefetch=1,
        grid=(q_tiles, k_tiles),
        in_specs=[
            pl.BlockSpec((QUERY_TILE, HEAD), lambda i, j, meta: (i, 0)),
            pl.BlockSpec((None, KEY_TILE, HEAD), key_map),
            pl.BlockSpec((None, KEY_TILE, HEAD), lambda i, j, meta: (1,) + key_map(i, j, meta)[1:]),
            row_spec,
            row_spec,
            row_spec,
            acc_spec,
        ],
        out_specs=[row_spec, row_spec, acc_spec],
    )
    return pl.pallas_call(
        flash_kernel,
        grid_spec=grid_spec,
        out_shape=[jax.ShapeDtypeStruct(s.shape, jnp.float32) for s in state],
        input_output_aliases={5: 0, 6: 1, 7: 2},
        compiler_params=pltpu.CompilerParams(
            dimension_semantics=("arbitrary", "arbitrary"), vmem_limit_bytes=48 * 1024 * 1024
        ),
    )(meta, queries, key_value, key_value, starts, *state)


def body(
    req_count,
    plane,
    tokens,
    input_norm_gain,
    query_weight,
    key_weight,
    value_weight,
    query_down_maps,
    value_down_maps,
    query_up_maps,
    value_up_maps,
    lengths,
    prompt_adapter_index,
):
    row_count = tokens.shape[0]
    req_index = lax.axis_index("req")
    positions = req_index * row_count + jnp.arange(row_count, dtype=jnp.int32)
    starts, prompt = prompt_layout(lengths, positions)
    causal_mask = adapter_mask(prompt, prompt_adapter_index, ADAPTER_COUNT, ADAPTER_RANK)
    incoming_weights = (query_weight, key_weight, value_weight, query_down_maps, value_down_maps)
    whole = lax.all_gather(tokens, "tp", axis=1, tiled=True)
    whole_float = whole.astype(jnp.float32)
    normed = (
        whole_float
        * lax.rsqrt(jnp.mean(whole_float * whole_float, axis=1, keepdims=True) + EPS)
        * input_norm_gain[None, :]
    ).astype(jnp.bfloat16)
    projected = tuple(
        (jnp.dot(normed, weight, preferred_element_type=jnp.float32) for weight in incoming_weights)
    )
    query_linear, key_lin, value_linear, query_middle, value_middle = projected
    query_middle = (query_middle * causal_mask).astype(jnp.bfloat16)
    value_middle = (value_middle * causal_mask).astype(jnp.bfloat16)
    query_linear = query_linear + ADAPTER_SCALE * jnp.dot(
        query_middle, query_up_maps, preferred_element_type=jnp.float32
    )
    value_rows = (
        value_linear
        + ADAPTER_SCALE * jnp.dot(value_middle, value_up_maps, preferred_element_type=jnp.float32)
    ).astype(jnp.bfloat16)
    head_count = query_linear.shape[1] // HEAD
    offsets = positions - starts
    queries = rotate(query_linear.reshape(row_count, head_count, HEAD), offsets, HEAD).astype(
        jnp.bfloat16
    )
    keys = rotate(key_lin.reshape(row_count, head_count, HEAD), offsets, HEAD).astype(jnp.bfloat16)
    values = value_rows.reshape(row_count, head_count, HEAD)
    scale = 1.0 / math.sqrt(HEAD)

    group = head_count
    span = group * row_count
    member = req_index % group
    chunk = req_index // group

    def group_pairs(step):
        return [
            (b * group + i, b * group + (i + step) % group)
            for b in range(req_count // group)
            for i in range(group)
        ]

    def regroup(parts, axis):
        order = (member - jnp.arange(group, dtype=jnp.int32)) % group
        return jnp.take(jnp.stack(parts), order, axis=axis)

    qkv = jnp.stack([queries, keys, values])
    parts = [lax.dynamic_index_in_dim(qkv, member, axis=2, keepdims=False)]
    for step in range(1, group):
        sent = lax.dynamic_index_in_dim(qkv, (member + step) % group, axis=2, keepdims=False)
        parts.append(lax.ppermute(sent, "req", group_pairs(step)))
    local = regroup(parts, 0)
    local = jnp.transpose(local, (1, 0, 2, 3)).reshape(3, span, HEAD)
    query_span = local[0]
    key_value = local[1:]

    chunk_count = req_count // group
    reach = MAXLEN - 1
    span_positions = chunk * span + jnp.arange(span, dtype=jnp.int32)
    span_starts, _ = prompt_layout(lengths, span_positions)
    span_starts = span_starts.reshape(span, 1)
    state = (
        jnp.full((span, 1), MASKED, jnp.float32),
        jnp.zeros((span, 1), jnp.float32),
        jnp.zeros((span, HEAD), jnp.float32),
    )
    arrived = [(key_value, chunk * span)]
    for back in range(1, chunk_count):
        if (back - 1) * span >= reach:
            break
        rows = min(span, -(-(reach - (back - 1) * span) // KEY_TILE) * KEY_TILE)
        shift = back * group
        sent = key_value[:, span - rows :]
        if shift == 2 * plane and req_count == 4 * plane:
            sources = range(req_count - shift)
            via = [(i - plane) % req_count for i in sources]
            sent = lax.ppermute(sent, "req", list(zip(sources, via)))
            segment = lax.ppermute(sent, "req", [(v, i + shift) for i, v in zip(sources, via)])
        else:
            pairs = [(i, i + shift) for i in range(req_count - shift)]
            segment = lax.ppermute(sent, "req", pairs)
        arrived.append((segment, (chunk - back) * span + span - rows))
    for segment, key_base in arrived:
        state = flash_step(state, query_span, span_starts, segment, chunk * span, key_base)
    peak, total, summed = state
    attended = (summed / total).astype(jnp.bfloat16)
    attended = attended.reshape(group, row_count, HEAD)

    parts = [lax.dynamic_index_in_dim(attended, member, axis=0, keepdims=False)]
    for step in range(1, group):
        sent = lax.dynamic_index_in_dim(attended, (member + step) % group, axis=0, keepdims=False)
        parts.append(lax.ppermute(sent, "req", group_pairs(step)))
    out = regroup(parts, 0)
    return jnp.transpose(out, (1, 0, 2)).reshape(row_count, head_count * HEAD)


def solution(mesh):
    in_specs = (
        P("req", "tp"),
        P(),
        P(None, "tp"),
        P(None, "tp"),
        P(None, "tp"),
        P(),
        P(),
        P(None, "tp"),
        P(None, "tp"),
        P(),
        P(),
    )
    out_specs = P("req", "tp")
    plane = mesh.shape["req"] // 4
    fn = functools.partial(body, mesh.shape["req"], plane)
    return jax.shard_map(fn, mesh=mesh, in_specs=in_specs, out_specs=out_specs, check_vma=False)
```

```python
import functools
import math

import jax
import jax.numpy as jnp
from jax import lax
from jax.experimental import pallas as pl
from jax.experimental.pallas import tpu as pltpu
from jax.sharding import PartitionSpec as P

HEAD = 128
ADAPTER_RANK = 16
ADAPTER_COUNT = 32


EPS = 1e-05
ADAPTER_SCALE = 0.5
MASKED = -1e30


def prompt_layout(lengths, positions):
    ends = jnp.cumsum(lengths)
    before = (ends[None, :] <= positions[:, None]).astype(jnp.int32)
    starts = jnp.sum(before * lengths[None, :], axis=1)
    prompt = jnp.sum(before, axis=1)
    return (starts, prompt)


def adapter_mask(prompt, prompt_adapter_index, count, rank):
    chosen = (
        prompt[:, None] == jnp.arange(prompt_adapter_index.shape[0], dtype=jnp.int32)[None, :]
    ).astype(jnp.int32)
    adapter = jnp.sum(chosen * prompt_adapter_index[None, :], axis=1)
    column = jnp.arange(count * rank, dtype=jnp.int32) // rank
    return (column[None, :] == adapter[:, None]).astype(jnp.float32)


def rotate(field, offsets, width):
    half = width // 2
    freq = jnp.exp(jnp.arange(half, dtype=jnp.float32) * (-2.0 * math.log(10000.0) / width))
    angle = offsets.astype(jnp.float32)[:, None] * freq[None, :]
    cosine = jnp.cos(angle)[:, None, :]
    sine = jnp.sin(angle)[:, None, :]
    first = field[..., :half]
    second = field[..., half:]
    return jnp.concatenate(
        [first * cosine - second * sine, second * cosine + first * sine], axis=-1
    )


MAXLEN = 8448

QUERY_TILE = 1024
KEY_TILE = 512


def flash_kernel(
    meta, q_ref, k_ref, v_ref, start_ref, peak_in, total_in, acc_in, peak_ref, total_ref, acc_ref
):
    i = pl.program_id(0)
    j = pl.program_id(1)
    q_tiles = pl.num_programs(0)
    lo = meta[2 + 2 * i]
    hi = meta[3 + 2 * i]

    @pl.when(j == 0)
    def _():
        peak_ref[...] = peak_in[...]
        total_ref[...] = total_in[...]
        acc_ref[...] = acc_in[...]

    block = lo + j
    active = block <= hi
    full = (block >= meta[2 + 2 * q_tiles + 2 * i]) & (block <= meta[3 + 2 * q_tiles + 2 * i])

    def update(masked):
        scores = lax.dot_general(
            q_ref[...], k_ref[...], (((1,), (1,)), ((), ())), preferred_element_type=jnp.float32
        ) * (1.0 / math.sqrt(HEAD))
        if masked:
            q_pos = meta[0] + i * QUERY_TILE + lax.broadcasted_iota(jnp.int32, (QUERY_TILE, 1), 0)
            k_pos = meta[1] + block * KEY_TILE + lax.broadcasted_iota(jnp.int32, (1, KEY_TILE), 1)
            allowed = (k_pos >= start_ref[...]) & (k_pos <= q_pos)
            scores = jnp.where(allowed, scores, MASKED)
        peak = peak_ref[...]
        new_peak = jnp.maximum(peak, jnp.max(scores, axis=1, keepdims=True))
        weights = jnp.exp(scores - new_peak)
        if masked:
            weights = jnp.where(allowed, weights, 0.0)
        factor = jnp.exp(peak - new_peak)
        total_ref[...] = total_ref[...] * factor + jnp.sum(weights, axis=1, keepdims=True)
        acc_ref[...] = acc_ref[...] * factor + jnp.dot(
            weights.astype(jnp.bfloat16), v_ref[...], preferred_element_type=jnp.float32
        )
        peak_ref[...] = new_peak

    @pl.when(active & full)
    def _():
        update(False)

    @pl.when(active & jnp.logical_not(full))
    def _():
        update(True)


def flash_step(state, queries, starts, key_value, query_first, key_base):
    query_rows = queries.shape[0]
    key_rows = key_value.shape[1]
    q_tiles = query_rows // QUERY_TILE
    k_tiles = key_rows // KEY_TILE
    positions = query_first + jnp.arange(query_rows, dtype=jnp.int32)
    tile_first = starts[::QUERY_TILE, 0]
    tile_last = positions[QUERY_TILE - 1 :: QUERY_TILE]
    lo = jnp.maximum((tile_first - key_base) // KEY_TILE, 0)
    hi = jnp.minimum((tile_last - key_base) // KEY_TILE, k_tiles - 1)
    tile_top = starts[QUERY_TILE - 1 :: QUERY_TILE, 0]
    tile_low = positions[::QUERY_TILE]
    full_lo = -((key_base - tile_top) // KEY_TILE)
    full_hi = (tile_low - (KEY_TILE - 1) - key_base) // KEY_TILE
    meta = jnp.concatenate(
        [
            jnp.stack([query_first, key_base]).astype(jnp.int32),
            jnp.stack([lo, hi], 1).reshape(-1),
            jnp.stack([full_lo, full_hi], 1).reshape(-1),
        ]
    ).astype(jnp.int32)

    def key_map(i, j, meta):
        block = jnp.minimum(meta[2 + 2 * i] + j, meta[3 + 2 * i])
        return (0, jnp.clip(block, 0, k_tiles - 1), 0)

    row_spec = pl.BlockSpec((QUERY_TILE, 1), lambda i, j, meta: (i, 0))
    acc_spec = pl.BlockSpec((QUERY_TILE, HEAD), lambda i, j, meta: (i, 0))
    grid_spec = pltpu.PrefetchScalarGridSpec(
        num_scalar_prefetch=1,
        grid=(q_tiles, k_tiles),
        in_specs=[
            pl.BlockSpec((QUERY_TILE, HEAD), lambda i, j, meta: (i, 0)),
            pl.BlockSpec((None, KEY_TILE, HEAD), key_map),
            pl.BlockSpec((None, KEY_TILE, HEAD), lambda i, j, meta: (1,) + key_map(i, j, meta)[1:]),
            row_spec,
            row_spec,
            row_spec,
            acc_spec,
        ],
        out_specs=[row_spec, row_spec, acc_spec],
    )
    return pl.pallas_call(
        flash_kernel,
        grid_spec=grid_spec,
        out_shape=[jax.ShapeDtypeStruct(s.shape, jnp.float32) for s in state],
        input_output_aliases={5: 0, 6: 1, 7: 2},
        compiler_params=pltpu.CompilerParams(
            dimension_semantics=("arbitrary", "arbitrary"), vmem_limit_bytes=48 * 1024 * 1024
        ),
    )(meta, queries, key_value, key_value, starts, *state)


def body(
    req_count,
    plane,
    tokens,
    input_norm_gain,
    query_weight,
    key_weight,
    value_weight,
    query_down_maps,
    value_down_maps,
    query_up_maps,
    value_up_maps,
    lengths,
    prompt_adapter_index,
):
    row_count = tokens.shape[0]
    req_index = lax.axis_index("req")
    positions = req_index * row_count + jnp.arange(row_count, dtype=jnp.int32)
    starts, prompt = prompt_layout(lengths, positions)
    causal_mask = adapter_mask(prompt, prompt_adapter_index, ADAPTER_COUNT, ADAPTER_RANK)
    incoming_weights = (query_weight, key_weight, value_weight, query_down_maps, value_down_maps)
    whole = lax.all_gather(tokens, "tp", axis=1, tiled=True)
    whole_float = whole.astype(jnp.float32)
    normed = (
        whole_float
        * lax.rsqrt(jnp.mean(whole_float * whole_float, axis=1, keepdims=True) + EPS)
        * input_norm_gain[None, :]
    ).astype(jnp.bfloat16)
    projected = tuple(
        (jnp.dot(normed, weight, preferred_element_type=jnp.float32) for weight in incoming_weights)
    )
    query_linear, key_lin, value_linear, query_middle, value_middle = projected
    query_middle = (query_middle * causal_mask).astype(jnp.bfloat16)
    value_middle = (value_middle * causal_mask).astype(jnp.bfloat16)
    query_linear = query_linear + ADAPTER_SCALE * jnp.dot(
        query_middle, query_up_maps, preferred_element_type=jnp.float32
    )
    value_rows = (
        value_linear
        + ADAPTER_SCALE * jnp.dot(value_middle, value_up_maps, preferred_element_type=jnp.float32)
    ).astype(jnp.bfloat16)
    head_count = query_linear.shape[1] // HEAD
    offsets = positions - starts
    queries = rotate(query_linear.reshape(row_count, head_count, HEAD), offsets, HEAD).astype(
        jnp.bfloat16
    )
    keys = rotate(key_lin.reshape(row_count, head_count, HEAD), offsets, HEAD).astype(jnp.bfloat16)
    values = value_rows.reshape(row_count, head_count, HEAD)
    scale = 1.0 / math.sqrt(HEAD)

    group = head_count
    span = group * row_count
    member = req_index % group
    chunk = req_index // group

    def group_pairs(step):
        return [
            (b * group + i, b * group + (i + step) % group)
            for b in range(req_count // group)
            for i in range(group)
        ]

    def regroup(parts, axis):
        order = (member - jnp.arange(group, dtype=jnp.int32)) % group
        return jnp.take(jnp.stack(parts), order, axis=axis)

    qkv = jnp.stack([queries, keys, values])
    parts = [lax.dynamic_index_in_dim(qkv, member, axis=2, keepdims=False)]
    for step in range(1, group):
        sent = lax.dynamic_index_in_dim(qkv, (member + step) % group, axis=2, keepdims=False)
        parts.append(lax.ppermute(sent, "req", group_pairs(step)))
    local = regroup(parts, 0)
    local = jnp.transpose(local, (1, 0, 2, 3)).reshape(3, span, HEAD)
    query_span = local[0]
    key_value = local[1:]

    chunk_count = req_count // group
    reach = MAXLEN - 1
    span_positions = chunk * span + jnp.arange(span, dtype=jnp.int32)
    span_starts, _ = prompt_layout(lengths, span_positions)
    span_starts = span_starts.reshape(span, 1)
    state = (
        jnp.full((span, 1), MASKED, jnp.float32),
        jnp.zeros((span, 1), jnp.float32),
        jnp.zeros((span, HEAD), jnp.float32),
    )
    arrived = [(key_value, chunk * span)]
    for back in range(1, chunk_count):
        if (back - 1) * span >= reach:
            break
        rows = min(span, -(-(reach - (back - 1) * span) // KEY_TILE) * KEY_TILE)
        shift = back * group
        sent = key_value[:, span - rows :]
        if shift == 2 * plane and req_count == 4 * plane:
            sources = range(req_count - shift)
            via = [(i - plane) % req_count for i in sources]
            sent = lax.ppermute(sent, "req", list(zip(sources, via)))
            segment = lax.ppermute(sent, "req", [(v, i + shift) for i, v in zip(sources, via)])
        else:
            pairs = [(i, i + shift) for i in range(req_count - shift)]
            segment = lax.ppermute(sent, "req", pairs)
        arrived.append((segment, (chunk - back) * span + span - rows))
    for segment, key_base in arrived:
        state = flash_step(state, query_span, span_starts, segment, chunk * span, key_base)
    peak, total, summed = state
    attended = (summed / total).astype(jnp.bfloat16)
    attended = attended.reshape(group, row_count, HEAD)

    parts = [lax.dynamic_index_in_dim(attended, member, axis=0, keepdims=False)]
    for step in range(1, group):
        sent = lax.dynamic_index_in_dim(attended, (member + step) % group, axis=0, keepdims=False)
        parts.append(lax.ppermute(sent, "req", group_pairs(step)))
    out = regroup(parts, 0)
    return jnp.transpose(out, (1, 0, 2)).reshape(row_count, head_count * HEAD)


def solution(mesh):
    in_specs = (
        P("req", "tp"),
        P(),
        P(None, "tp"),
        P(None, "tp"),
        P(None, "tp"),
        P(),
        P(),
        P(None, "tp"),
        P(None, "tp"),
        P(),
        P(),
    )
    out_specs = P("req", "tp")
    plane = mesh.shape["req"] // 4
    fn = functools.partial(body, mesh.shape["req"], plane)
    return jax.shard_map(fn, mesh=mesh, in_specs=in_specs, out_specs=out_specs, check_vma=False)
```

```python
import functools
import math

import jax
import jax.numpy as jnp
from jax import lax
from jax.experimental import pallas as pl
from jax.experimental.pallas import tpu as pltpu
from jax.sharding import PartitionSpec as P

HEAD = 128
ADAPTER_RANK = 16
ADAPTER_COUNT = 32


EPS = 1e-05
ADAPTER_SCALE = 0.5
MASKED = -1e30


def prompt_layout(lengths, positions):
    ends = jnp.cumsum(lengths)
    before = (ends[None, :] <= positions[:, None]).astype(jnp.int32)
    starts = jnp.sum(before * lengths[None, :], axis=1)
    prompt = jnp.sum(before, axis=1)
    return (starts, prompt)


def adapter_mask(prompt, prompt_adapter_index, count, rank):
    chosen = (
        prompt[:, None] == jnp.arange(prompt_adapter_index.shape[0], dtype=jnp.int32)[None, :]
    ).astype(jnp.int32)
    adapter = jnp.sum(chosen * prompt_adapter_index[None, :], axis=1)
    column = jnp.arange(count * rank, dtype=jnp.int32) // rank
    return (column[None, :] == adapter[:, None]).astype(jnp.float32)


def rotate(field, offsets, width):
    half = width // 2
    freq = jnp.exp(jnp.arange(half, dtype=jnp.float32) * (-2.0 * math.log(10000.0) / width))
    angle = offsets.astype(jnp.float32)[:, None] * freq[None, :]
    cosine = jnp.cos(angle)[:, None, :]
    sine = jnp.sin(angle)[:, None, :]
    first = field[..., :half]
    second = field[..., half:]
    return jnp.concatenate(
        [first * cosine - second * sine, second * cosine + first * sine], axis=-1
    )


MAXLEN = 8448

QUERY_TILE = 1024
KEY_TILE = 512


def flash_kernel(
    meta, q_ref, k_ref, v_ref, start_ref, peak_in, total_in, acc_in, peak_ref, total_ref, acc_ref
):
    i = pl.program_id(0)
    j = pl.program_id(1)
    lo = meta[2 + 2 * i]
    hi = meta[3 + 2 * i]

    @pl.when(j == 0)
    def _():
        peak_ref[...] = peak_in[...]
        total_ref[...] = total_in[...]
        acc_ref[...] = acc_in[...]

    @pl.when(lo + j <= hi)
    def _():
        block = lo + j
        scores = lax.dot_general(
            q_ref[...], k_ref[...], (((1,), (1,)), ((), ())), preferred_element_type=jnp.float32
        ) * (1.0 / math.sqrt(HEAD))
        q_pos = meta[0] + i * QUERY_TILE + lax.broadcasted_iota(jnp.int32, (QUERY_TILE, 1), 0)
        k_pos = meta[1] + block * KEY_TILE + lax.broadcasted_iota(jnp.int32, (1, KEY_TILE), 1)
        allowed = (k_pos >= start_ref[...]) & (k_pos <= q_pos)
        scores = jnp.where(allowed, scores, MASKED)
        peak = peak_ref[...]
        new_peak = jnp.maximum(peak, jnp.max(scores, axis=1, keepdims=True))
        weights = jnp.where(allowed, jnp.exp(scores - new_peak), 0.0)
        factor = jnp.exp(peak - new_peak)
        total_ref[...] = total_ref[...] * factor + jnp.sum(weights, axis=1, keepdims=True)
        acc_ref[...] = acc_ref[...] * factor + jnp.dot(
            weights.astype(jnp.bfloat16), v_ref[...], preferred_element_type=jnp.float32
        )
        peak_ref[...] = new_peak


def flash_step(state, queries, starts, key_value, query_first, key_base):
    query_rows = queries.shape[0]
    key_rows = key_value.shape[1]
    q_tiles = query_rows // QUERY_TILE
    k_tiles = key_rows // KEY_TILE
    positions = query_first + jnp.arange(query_rows, dtype=jnp.int32)
    tile_first = starts[::QUERY_TILE, 0]
    tile_last = positions[QUERY_TILE - 1 :: QUERY_TILE]
    lo = jnp.maximum((tile_first - key_base) // KEY_TILE, 0)
    hi = jnp.minimum((tile_last - key_base) // KEY_TILE, k_tiles - 1)
    meta = jnp.concatenate(
        [jnp.stack([query_first, key_base]).astype(jnp.int32), jnp.stack([lo, hi], 1).reshape(-1)]
    ).astype(jnp.int32)

    def key_map(i, j, meta):
        block = jnp.minimum(meta[2 + 2 * i] + j, meta[3 + 2 * i])
        return (0, jnp.clip(block, 0, k_tiles - 1), 0)

    row_spec = pl.BlockSpec((QUERY_TILE, 1), lambda i, j, meta: (i, 0))
    acc_spec = pl.BlockSpec((QUERY_TILE, HEAD), lambda i, j, meta: (i, 0))
    grid_spec = pltpu.PrefetchScalarGridSpec(
        num_scalar_prefetch=1,
        grid=(q_tiles, k_tiles),
        in_specs=[
            pl.BlockSpec((QUERY_TILE, HEAD), lambda i, j, meta: (i, 0)),
            pl.BlockSpec((None, KEY_TILE, HEAD), key_map),
            pl.BlockSpec((None, KEY_TILE, HEAD), lambda i, j, meta: (1,) + key_map(i, j, meta)[1:]),
            row_spec,
            row_spec,
            row_spec,
            acc_spec,
        ],
        out_specs=[row_spec, row_spec, acc_spec],
    )
    return pl.pallas_call(
        flash_kernel,
        grid_spec=grid_spec,
        out_shape=[jax.ShapeDtypeStruct(s.shape, jnp.float32) for s in state],
        input_output_aliases={5: 0, 6: 1, 7: 2},
        compiler_params=pltpu.CompilerParams(
            dimension_semantics=("arbitrary", "arbitrary"), vmem_limit_bytes=48 * 1024 * 1024
        ),
    )(meta, queries, key_value, key_value, starts, *state)


def body(
    req_count,
    plane,
    tokens,
    input_norm_gain,
    query_weight,
    key_weight,
    value_weight,
    query_down_maps,
    value_down_maps,
    query_up_maps,
    value_up_maps,
    lengths,
    prompt_adapter_index,
):
    row_count = tokens.shape[0]
    req_index = lax.axis_index("req")
    positions = req_index * row_count + jnp.arange(row_count, dtype=jnp.int32)
    starts, prompt = prompt_layout(lengths, positions)
    causal_mask = adapter_mask(prompt, prompt_adapter_index, ADAPTER_COUNT, ADAPTER_RANK)
    incoming_weights = (query_weight, key_weight, value_weight, query_down_maps, value_down_maps)
    whole = lax.all_gather(tokens, "tp", axis=1, tiled=True)
    whole_float = whole.astype(jnp.float32)
    normed = (
        whole_float
        * lax.rsqrt(jnp.mean(whole_float * whole_float, axis=1, keepdims=True) + EPS)
        * input_norm_gain[None, :]
    ).astype(jnp.bfloat16)
    projected = tuple(
        (jnp.dot(normed, weight, preferred_element_type=jnp.float32) for weight in incoming_weights)
    )
    query_linear, key_lin, value_linear, query_middle, value_middle = projected
    query_middle = (query_middle * causal_mask).astype(jnp.bfloat16)
    value_middle = (value_middle * causal_mask).astype(jnp.bfloat16)
    query_linear = query_linear + ADAPTER_SCALE * jnp.dot(
        query_middle, query_up_maps, preferred_element_type=jnp.float32
    )
    value_rows = (
        value_linear
        + ADAPTER_SCALE * jnp.dot(value_middle, value_up_maps, preferred_element_type=jnp.float32)
    ).astype(jnp.bfloat16)
    head_count = query_linear.shape[1] // HEAD
    offsets = positions - starts
    queries = rotate(query_linear.reshape(row_count, head_count, HEAD), offsets, HEAD).astype(
        jnp.bfloat16
    )
    keys = rotate(key_lin.reshape(row_count, head_count, HEAD), offsets, HEAD).astype(jnp.bfloat16)
    values = value_rows.reshape(row_count, head_count, HEAD)
    scale = 1.0 / math.sqrt(HEAD)

    group = head_count
    span = group * row_count
    member = req_index % group
    chunk = req_index // group

    def group_pairs(step):
        return [
            (b * group + i, b * group + (i + step) % group)
            for b in range(req_count // group)
            for i in range(group)
        ]

    def regroup(parts, axis):
        order = (member - jnp.arange(group, dtype=jnp.int32)) % group
        return jnp.take(jnp.stack(parts), order, axis=axis)

    def trade(stacked):
        parts = [lax.dynamic_index_in_dim(stacked, member, axis=2, keepdims=False)]
        for step in range(1, group):
            sent = lax.dynamic_index_in_dim(stacked, (member + step) % group, axis=2, keepdims=False)
            parts.append(lax.ppermute(sent, "req", group_pairs(step)))
        local = regroup(parts, 0)
        return jnp.transpose(local, (1, 0, 2, 3)).reshape(stacked.shape[0], span, HEAD)

    key_value = trade(jnp.stack([keys, values]))
    query_span = trade(queries[None])[0]

    chunk_count = req_count // group
    reach = MAXLEN - 1
    span_positions = chunk * span + jnp.arange(span, dtype=jnp.int32)
    span_starts, _ = prompt_layout(lengths, span_positions)
    span_starts = span_starts.reshape(span, 1)
    state = (
        jnp.full((span, 1), MASKED, jnp.float32),
        jnp.zeros((span, 1), jnp.float32),
        jnp.zeros((span, HEAD), jnp.float32),
    )
    arrived = [(key_value, chunk * span)]
    for back in range(1, chunk_count):
        if (back - 1) * span >= reach:
            break
        rows = min(span, -(-(reach - (back - 1) * span) // KEY_TILE) * KEY_TILE)
        shift = back * group
        sent = key_value[:, span - rows :]
        if shift == 2 * plane and req_count == 4 * plane:
            sources = range(req_count - shift)
            via = [(i - plane) % req_count for i in sources]
            sent = lax.ppermute(sent, "req", list(zip(sources, via)))
            segment = lax.ppermute(sent, "req", [(v, i + shift) for i, v in zip(sources, via)])
        else:
            pairs = [(i, i + shift) for i in range(req_count - shift)]
            segment = lax.ppermute(sent, "req", pairs)
        arrived.append((segment, (chunk - back) * span + span - rows))
    for segment, key_base in arrived:
        state = flash_step(state, query_span, span_starts, segment, chunk * span, key_base)
    peak, total, summed = state
    attended = (summed / total).astype(jnp.bfloat16)
    attended = attended.reshape(group, row_count, HEAD)

    parts = [lax.dynamic_index_in_dim(attended, member, axis=0, keepdims=False)]
    for step in range(1, group):
        sent = lax.dynamic_index_in_dim(attended, (member + step) % group, axis=0, keepdims=False)
        parts.append(lax.ppermute(sent, "req", group_pairs(step)))
    out = regroup(parts, 0)
    return jnp.transpose(out, (1, 0, 2)).reshape(row_count, head_count * HEAD)


def solution(mesh):
    in_specs = (
        P("req", "tp"),
        P(),
        P(None, "tp"),
        P(None, "tp"),
        P(None, "tp"),
        P(),
        P(),
        P(None, "tp"),
        P(None, "tp"),
        P(),
        P(),
    )
    out_specs = P("req", "tp")
    plane = mesh.shape["req"] // 4
    fn = functools.partial(body, mesh.shape["req"], plane)
    return jax.shard_map(fn, mesh=mesh, in_specs=in_specs, out_specs=out_specs, check_vma=False)
```

```python
import functools
import math

import jax
import jax.numpy as jnp
from jax import lax
from jax.experimental import pallas as pl
from jax.experimental.pallas import tpu as pltpu
from jax.sharding import PartitionSpec as P

HEAD = 128
ADAPTER_RANK = 16
ADAPTER_COUNT = 32


EPS = 1e-05
ADAPTER_SCALE = 0.5
MASKED = -1e30


def prompt_layout(lengths, positions):
    ends = jnp.cumsum(lengths)
    before = (ends[None, :] <= positions[:, None]).astype(jnp.int32)
    starts = jnp.sum(before * lengths[None, :], axis=1)
    prompt = jnp.sum(before, axis=1)
    return (starts, prompt)


def adapter_mask(prompt, prompt_adapter_index, count, rank):
    chosen = (
        prompt[:, None] == jnp.arange(prompt_adapter_index.shape[0], dtype=jnp.int32)[None, :]
    ).astype(jnp.int32)
    adapter = jnp.sum(chosen * prompt_adapter_index[None, :], axis=1)
    column = jnp.arange(count * rank, dtype=jnp.int32) // rank
    return (column[None, :] == adapter[:, None]).astype(jnp.float32)


def rotate(field, offsets, width):
    half = width // 2
    freq = jnp.exp(jnp.arange(half, dtype=jnp.float32) * (-2.0 * math.log(10000.0) / width))
    angle = offsets.astype(jnp.float32)[:, None] * freq[None, :]
    cosine = jnp.cos(angle)[:, None, :]
    sine = jnp.sin(angle)[:, None, :]
    first = field[..., :half]
    second = field[..., half:]
    return jnp.concatenate(
        [first * cosine - second * sine, second * cosine + first * sine], axis=-1
    )


MAXLEN = 8448

QUERY_TILE = 1024
KEY_TILE = 512


def flash_kernel(
    meta, q_ref, k_ref, v_ref, start_ref, peak_in, total_in, acc_in, peak_ref, total_ref, acc_ref
):
    i = pl.program_id(0)
    j = pl.program_id(1)
    lo = meta[2 + 2 * i]
    hi = meta[3 + 2 * i]

    @pl.when(j == 0)
    def _():
        peak_ref[...] = peak_in[...]
        total_ref[...] = total_in[...]
        acc_ref[...] = acc_in[...]

    @pl.when(lo + j <= hi)
    def _():
        block = lo + j
        scores = lax.dot_general(
            q_ref[...], k_ref[...], (((1,), (1,)), ((), ())), preferred_element_type=jnp.float32
        ) * (1.0 / math.sqrt(HEAD))
        q_pos = meta[0] + i * QUERY_TILE + lax.broadcasted_iota(jnp.int32, (QUERY_TILE, 1), 0)
        k_pos = meta[1] + block * KEY_TILE + lax.broadcasted_iota(jnp.int32, (1, KEY_TILE), 1)
        allowed = (k_pos >= start_ref[...]) & (k_pos <= q_pos)
        scores = jnp.where(allowed, scores, -jnp.inf)
        peak = peak_ref[...]
        new_peak = jnp.maximum(peak, jnp.max(scores, axis=1, keepdims=True))
        weights = jnp.exp(scores - new_peak)
        factor = jnp.exp(peak - new_peak)
        total_ref[...] = total_ref[...] * factor + jnp.sum(weights, axis=1, keepdims=True)
        acc_ref[...] = acc_ref[...] * factor + jnp.dot(
            weights.astype(jnp.bfloat16), v_ref[...], preferred_element_type=jnp.float32
        )
        peak_ref[...] = new_peak


def flash_step(state, queries, starts, key_value, query_first, key_base):
    query_rows = queries.shape[0]
    key_rows = key_value.shape[1]
    q_tiles = query_rows // QUERY_TILE
    k_tiles = key_rows // KEY_TILE
    positions = query_first + jnp.arange(query_rows, dtype=jnp.int32)
    tile_first = starts[::QUERY_TILE, 0]
    tile_last = positions[QUERY_TILE - 1 :: QUERY_TILE]
    lo = jnp.maximum((tile_first - key_base) // KEY_TILE, 0)
    hi = jnp.minimum((tile_last - key_base) // KEY_TILE, k_tiles - 1)
    meta = jnp.concatenate(
        [jnp.stack([query_first, key_base]).astype(jnp.int32), jnp.stack([lo, hi], 1).reshape(-1)]
    ).astype(jnp.int32)

    def key_map(i, j, meta):
        block = jnp.minimum(meta[2 + 2 * i] + j, meta[3 + 2 * i])
        return (0, jnp.clip(block, 0, k_tiles - 1), 0)

    row_spec = pl.BlockSpec((QUERY_TILE, 1), lambda i, j, meta: (i, 0))
    acc_spec = pl.BlockSpec((QUERY_TILE, HEAD), lambda i, j, meta: (i, 0))
    grid_spec = pltpu.PrefetchScalarGridSpec(
        num_scalar_prefetch=1,
        grid=(q_tiles, k_tiles),
        in_specs=[
            pl.BlockSpec((QUERY_TILE, HEAD), lambda i, j, meta: (i, 0)),
            pl.BlockSpec((None, KEY_TILE, HEAD), key_map),
            pl.BlockSpec((None, KEY_TILE, HEAD), lambda i, j, meta: (1,) + key_map(i, j, meta)[1:]),
            row_spec,
            row_spec,
            row_spec,
            acc_spec,
        ],
        out_specs=[row_spec, row_spec, acc_spec],
    )
    return pl.pallas_call(
        flash_kernel,
        grid_spec=grid_spec,
        out_shape=[jax.ShapeDtypeStruct(s.shape, jnp.float32) for s in state],
        input_output_aliases={5: 0, 6: 1, 7: 2},
        compiler_params=pltpu.CompilerParams(
            dimension_semantics=("arbitrary", "arbitrary"), vmem_limit_bytes=48 * 1024 * 1024
        ),
    )(meta, queries, key_value, key_value, starts, *state)


def body(
    req_count,
    plane,
    tokens,
    input_norm_gain,
    query_weight,
    key_weight,
    value_weight,
    query_down_maps,
    value_down_maps,
    query_up_maps,
    value_up_maps,
    lengths,
    prompt_adapter_index,
):
    row_count = tokens.shape[0]
    req_index = lax.axis_index("req")
    positions = req_index * row_count + jnp.arange(row_count, dtype=jnp.int32)
    starts, prompt = prompt_layout(lengths, positions)
    causal_mask = adapter_mask(prompt, prompt_adapter_index, ADAPTER_COUNT, ADAPTER_RANK)
    incoming_weights = (query_weight, key_weight, value_weight, query_down_maps, value_down_maps)
    whole = lax.all_gather(tokens, "tp", axis=1, tiled=True)
    whole_float = whole.astype(jnp.float32)
    normed = (
        whole_float
        * lax.rsqrt(jnp.mean(whole_float * whole_float, axis=1, keepdims=True) + EPS)
        * input_norm_gain[None, :]
    ).astype(jnp.bfloat16)
    projected = tuple(
        (jnp.dot(normed, weight, preferred_element_type=jnp.float32) for weight in incoming_weights)
    )
    query_linear, key_lin, value_linear, query_middle, value_middle = projected
    query_middle = (query_middle * causal_mask).astype(jnp.bfloat16)
    value_middle = (value_middle * causal_mask).astype(jnp.bfloat16)
    query_linear = query_linear + ADAPTER_SCALE * jnp.dot(
        query_middle, query_up_maps, preferred_element_type=jnp.float32
    )
    value_rows = (
        value_linear
        + ADAPTER_SCALE * jnp.dot(value_middle, value_up_maps, preferred_element_type=jnp.float32)
    ).astype(jnp.bfloat16)
    head_count = query_linear.shape[1] // HEAD
    offsets = positions - starts
    queries = rotate(query_linear.reshape(row_count, head_count, HEAD), offsets, HEAD).astype(
        jnp.bfloat16
    )
    keys = rotate(key_lin.reshape(row_count, head_count, HEAD), offsets, HEAD).astype(jnp.bfloat16)
    values = value_rows.reshape(row_count, head_count, HEAD)
    scale = 1.0 / math.sqrt(HEAD)

    group = head_count
    span = group * row_count
    member = req_index % group
    chunk = req_index // group

    def group_pairs(step):
        return [
            (b * group + i, b * group + (i + step) % group)
            for b in range(req_count // group)
            for i in range(group)
        ]

    def regroup(parts, axis):
        order = (member - jnp.arange(group, dtype=jnp.int32)) % group
        return jnp.take(jnp.stack(parts), order, axis=axis)

    def trade(stacked):
        parts = [lax.dynamic_index_in_dim(stacked, member, axis=2, keepdims=False)]
        for step in range(1, group):
            sent = lax.dynamic_index_in_dim(stacked, (member + step) % group, axis=2, keepdims=False)
            parts.append(lax.ppermute(sent, "req", group_pairs(step)))
        local = regroup(parts, 0)
        return jnp.transpose(local, (1, 0, 2, 3)).reshape(stacked.shape[0], span, HEAD)

    key_value = trade(jnp.stack([keys, values]))
    query_span = trade(queries[None])[0]

    chunk_count = req_count // group
    reach = MAXLEN - 1
    span_positions = chunk * span + jnp.arange(span, dtype=jnp.int32)
    span_starts, _ = prompt_layout(lengths, span_positions)
    span_starts = span_starts.reshape(span, 1)
    state = (
        jnp.full((span, 1), MASKED, jnp.float32),
        jnp.zeros((span, 1), jnp.float32),
        jnp.zeros((span, HEAD), jnp.float32),
    )
    arrived = [(key_value, chunk * span)]
    for back in range(1, chunk_count):
        if (back - 1) * span >= reach:
            break
        rows = min(span, -(-(reach - (back - 1) * span) // KEY_TILE) * KEY_TILE)
        shift = back * group
        sent = key_value[:, span - rows :]
        if shift == 2 * plane and req_count == 4 * plane:
            sources = range(req_count - shift)
            via = [(i - plane) % req_count for i in sources]
            sent = lax.ppermute(sent, "req", list(zip(sources, via)))
            segment = lax.ppermute(sent, "req", [(v, i + shift) for i, v in zip(sources, via)])
        else:
            pairs = [(i, i + shift) for i in range(req_count - shift)]
            segment = lax.ppermute(sent, "req", pairs)
        arrived.append((segment, (chunk - back) * span + span - rows))
    for segment, key_base in arrived:
        state = flash_step(state, query_span, span_starts, segment, chunk * span, key_base)
    peak, total, summed = state
    attended = (summed / total).astype(jnp.bfloat16)
    attended = attended.reshape(group, row_count, HEAD)

    parts = [lax.dynamic_index_in_dim(attended, member, axis=0, keepdims=False)]
    for step in range(1, group):
        sent = lax.dynamic_index_in_dim(attended, (member + step) % group, axis=0, keepdims=False)
        parts.append(lax.ppermute(sent, "req", group_pairs(step)))
    out = regroup(parts, 0)
    return jnp.transpose(out, (1, 0, 2)).reshape(row_count, head_count * HEAD)


def solution(mesh):
    in_specs = (
        P("req", "tp"),
        P(),
        P(None, "tp"),
        P(None, "tp"),
        P(None, "tp"),
        P(),
        P(),
        P(None, "tp"),
        P(None, "tp"),
        P(),
        P(),
    )
    out_specs = P("req", "tp")
    plane = mesh.shape["req"] // 4
    fn = functools.partial(body, mesh.shape["req"], plane)
    return jax.shard_map(fn, mesh=mesh, in_specs=in_specs, out_specs=out_specs, check_vma=False)
```
